256 devices in a mesh: dp: 32 (over x_lo, z, core), blk: 8 (over y, x_hi).
Axes of the slice: x: 4 (x_hi: 2, x_lo: 2; x = x_hi * 2 + x_lo), y: 4, z: 8, core: 2. Of those that a mesh axis runs over, the one named last changes fastest.
Arguments:
- inputs: bfloat16 [8, 16384, 4096], P('blk', 'dp'), may hold values from -6 to 6
- out_grads: bfloat16 [8, 16384, 4096], P('blk', 'dp'), may hold values from -8 to 8
- test_matrix: bfloat16 [8, 4096, 256], P('blk'), may hold values from -6 to 6
- momentum: bfloat16 [8, 4096, 4096], P(None, 'blk', 'dp'), may hold values from -6 to 6
Outputs:
- update: bfloat16 [8, 4096, 4096], P(None, 'blk', 'dp')
The draws below stay inside these ranges and needn't reach their ends.
All inputs are finite; a program needn't handle non-finite values.
Results may differ from the reference program's by a relative error of at most 0.0035.
Values may be sent and summed in bfloat16 or wider, within the bound.
No kernel may reach another device: no remote copies, remote signals or barrier semaphores. Data moves between devices by JAX's collectives and lax.ppermute only.
A program may use at most 128 MiB of HBM per device.

```python
import jax
import jax.numpy as jnp
from jax import lax

BLOCK = 4096
RANK = 256
TOK_DEV = 512
REPLICAS = 32
BLOCKS = 8
TOKENS = 16384


def draw_out_grads(key, part):
    replica = (jnp.arange(TOKENS) // TOK_DEV).astype(jnp.float32)
    position = replica / (REPLICAS - 1.0)
    values = jnp.clip(jax.random.normal(key, (BLOCKS, TOKENS, BLOCK), jnp.float32), -6.0, 6.0)
    weights = jnp.exp(position * 1.0986123)
    row_scale = jnp.sqrt(weights / 1.8204784)
    scaled = values * row_scale[None, :, None]
    return jnp.clip(scaled, -8.0, 8.0).astype(jnp.bfloat16)


def level_of(rng, dims, split, smallest, top_value):
    level, own = 1.0, jax.random.fold_in(rng, 6)
    for dim, shards_of in split:
        draws = jnp.exp(jax.random.uniform(jax.random.fold_in(own, dim), (shards_of,), jnp.float32, smallest / len(split), top_value / len(split)))
        level = level * jnp.repeat(draws, dims[dim] // shards_of).reshape([-1 if axis == dim else 1 for axis in range(len(dims))])
    return level


def gaussian(own_key, dims, deviation, limit, shards=(), held_as=jnp.bfloat16):
    factor_of = level_of(own_key, dims, shards, -0.22, 0.18) if shards else 1.0
    array = jax.random.normal(own_key, dims, jnp.float32) * deviation * factor_of
    return jnp.minimum(jnp.maximum(array, -limit), limit).astype(held_as)


def setup_inputs(seed: int = 0) -> dict:
    streams_of = jax.random.split(jax.random.key(seed), 5)
    inputs = gaussian(streams_of[0], (BLOCKS, TOKENS, BLOCK), 1.0, 6.0, ((0, 8), (1, 32)))
    out_grads = draw_out_grads(jax.random.fold_in(streams_of[4], 71), 0)
    test_matrix = gaussian(streams_of[2], (BLOCKS, BLOCK, RANK), 1.0, 6.0, ((0, 8),))
    momentum = gaussian(streams_of[3], (BLOCKS, BLOCK, BLOCK), 1.0, 6.0, ((1, 8), (2, 32)))
    return {"inputs": inputs, "out_grads": out_grads, "test_matrix": test_matrix, "momentum": momentum}


def inner_gram(columns):
    return lax.dot_general(columns, columns, (((0,), (0,)), ((), ())), precision=lax.Precision.HIGHEST)

def cholesky_pass(columns, gram_matrix):
    lower_factor = jnp.linalg.cholesky(gram_matrix)
    return lax.linalg.triangular_solve(lower_factor, columns, left_side=False, lower=True, transpose_a=True)

def block_update(operands):
    features, errors, probes, moment_block = operands
    scale = 1.0 / (BLOCK * TOKENS)
    projected = jnp.dot(features.astype(jnp.float32), probes.astype(jnp.float32), preferred_element_type=jnp.float32).astype(jnp.bfloat16)
    grouped = errors.reshape(REPLICAS, TOK_DEV, BLOCK).astype(jnp.float32)
    token_gram = jnp.einsum('dtb,dsb->dts', grouped, grouped, precision=lax.Precision.HIGHEST).astype(jnp.bfloat16)
    gram_wide = token_gram.astype(jnp.float32)
    proj_wide = projected.reshape(REPLICAS, TOK_DEV, RANK).astype(jnp.float32)
    mixed_rows = jnp.einsum('dts,dsr->dtr', gram_wide, proj_wide, precision=lax.Precision.HIGHEST).astype(jnp.bfloat16)
    sketch = lax.dot_general(features.astype(jnp.float32), mixed_rows.reshape(TOKENS, RANK).astype(jnp.float32), (((0,), (0,)), ((), ())), preferred_element_type=jnp.float32) * scale
    basis = cholesky_pass(sketch, inner_gram(sketch)).astype(jnp.bfloat16)
    reduced = jnp.dot(features.astype(jnp.float32), basis.astype(jnp.float32), preferred_element_type=jnp.float32).astype(jnp.bfloat16)
    red_wide = reduced.reshape(REPLICAS, TOK_DEV, RANK).astype(jnp.float32)
    shaped = jnp.einsum('dts,dsr->dtr', gram_wide, red_wide, precision=lax.Precision.HIGHEST).astype(jnp.bfloat16)
    core_matrix = lax.dot_general(reduced.astype(jnp.float32), shaped.reshape(TOKENS, RANK).astype(jnp.float32), (((0,), (0,)), ((), ())), preferred_element_type=jnp.float32) * scale
    shifted = core_matrix + jnp.eye(RANK, dtype=jnp.float32)
    lower_factor = jnp.linalg.cholesky(shifted)
    half_solved = lax.linalg.triangular_solve(lower_factor, core_matrix, left_side=True, lower=True)
    factor = lax.linalg.triangular_solve(lower_factor, half_solved, left_side=True, lower=True, transpose_a=True)
    coeffs = lax.dot_general(basis.astype(jnp.float32), moment_block.astype(jnp.float32), (((0,), (0,)), ((), ())), preferred_element_type=jnp.float32)
    scaled = jnp.dot(factor, coeffs, precision=lax.Precision.HIGHEST).astype(jnp.bfloat16)
    fresh = moment_block.astype(jnp.float32) - jnp.dot(basis.astype(jnp.float32), scaled.astype(jnp.float32), preferred_element_type=jnp.float32)
    return fresh.astype(jnp.bfloat16)

def reference(inputs, out_grads, test_matrix, momentum):
    return lax.map(block_update, (inputs, out_grads, test_matrix, momentum))
```

```python
import jax
import jax.numpy as jnp
from jax import lax
from jax.sharding import PartitionSpec as P


def inner_gram(columns):
    return lax.dot_general(
        columns, columns, (((0,), (0,)), ((), ())), precision=lax.Precision.HIGHEST
    )


def cholesky_pass(columns, gram_matrix):
    lower_factor = jnp.linalg.cholesky(gram_matrix)
    return lax.linalg.triangular_solve(
        lower_factor, columns, left_side=False, lower=True, transpose_a=True
    )


def shards(inputs, out_grads, test_matrix, momentum):
    features = inputs[0]
    errors = out_grads[0]
    probes = test_matrix[0]
    replicas = lax.axis_size("dp")
    scale = 1.0 / (features.shape[1] * features.shape[0] * replicas)
    columns = lax.all_to_all(momentum, "blk", split_axis=0, concat_axis=1, tiled=True)[0]
    projected = jnp.dot(features, probes, preferred_element_type=jnp.float32).astype(jnp.bfloat16)
    token_gram = lax.dot_general(
        errors, errors, (((1,), (1,)), ((), ())), preferred_element_type=jnp.float32
    ).astype(jnp.bfloat16)
    mixed_rows = jnp.dot(token_gram, projected, preferred_element_type=jnp.float32).astype(
        jnp.bfloat16
    )
    sketch_term = (
        lax.dot_general(
            features, mixed_rows, (((0,), (0,)), ((), ())), preferred_element_type=jnp.float32
        )
        * scale
    )
    sketch = lax.psum(sketch_term, "dp")
    basis = cholesky_pass(sketch, inner_gram(sketch)).astype(jnp.bfloat16)
    reduced = jnp.dot(features, basis, preferred_element_type=jnp.float32).astype(jnp.bfloat16)
    shaped = jnp.dot(token_gram, reduced, preferred_element_type=jnp.float32).astype(jnp.bfloat16)
    core_term = (
        lax.dot_general(
            reduced, shaped, (((0,), (0,)), ((), ())), preferred_element_type=jnp.float32
        )
        * scale
    )
    core_matrix = lax.psum(core_term, "dp")
    shifted = core_matrix + jnp.eye(core_matrix.shape[0], dtype=jnp.float32)
    lower_factor = jnp.linalg.cholesky(shifted)
    half_solved = lax.linalg.triangular_solve(lower_factor, core_matrix, left_side=True, lower=True)
    factor = lax.linalg.triangular_solve(
        lower_factor, half_solved, left_side=True, lower=True, transpose_a=True
    )
    coeffs = lax.dot_general(
        basis, columns, (((0,), (0,)), ((), ())), preferred_element_type=jnp.float32
    )
    scaled = jnp.dot(factor, coeffs, precision=lax.Precision.HIGHEST).astype(jnp.bfloat16)
    fresh = (
        columns.astype(jnp.float32) - jnp.dot(basis, scaled, preferred_element_type=jnp.float32)
    ).astype(jnp.bfloat16)
    return lax.all_to_all(fresh[None], "blk", split_axis=1, concat_axis=0, tiled=True)


def solution(mesh):
    in_specs = (P("blk", "dp", None), P("blk", "dp", None), P("blk", None, None), P(None, "blk", "dp"))
    out_specs = P(None, "blk", "dp")
    return jax.shard_map(
        shards, mesh=mesh, in_specs=in_specs, out_specs=out_specs, check_vma=False
    )
```

```python
import jax
import jax.numpy as jnp
from jax import lax
from jax.sharding import Mesh
from jax.sharding import PartitionSpec as P

DP = ("dp_0", "dp_1", "dp_2")


def filled_up(lines, devices):
    spare = -len(lines) % devices
    return jnp.pad(lines, [(0, spare)] + [(0, 0)] * (lines.ndim - 1))


def copy_for_each(x, axis):
    devices = lax.axis_size(axis)
    return lax.all_to_all(jnp.broadcast_to(x[None], (devices, *x.shape)), axis, 0, 0, tiled=True)


def in_order(blocks, dim):
    blocks = jnp.moveaxis(blocks, 0, dim)
    lengths = blocks.shape
    return blocks.reshape(*lengths[:dim], lengths[dim] * lengths[dim + 1], *lengths[dim + 2 :])


def whole_of(x, axes, dim):
    far, near = axes
    first = copy_for_each(x, far)
    blocks = jnp.swapaxes(copy_for_each(first, near), 0, 1)
    return in_order(blocks.reshape(-1, *x.shape), dim)


def in_blocks(x, dim, devices):
    lengths = x.shape
    blocks = x.reshape(*lengths[:dim], devices, lengths[dim] // devices, *lengths[dim + 1 :])
    return jnp.moveaxis(blocks, dim, 0)


def sum_at_owner(x, axis, dim):
    blocks = in_blocks(x, dim, lax.axis_size(axis))
    arrived = lax.all_to_all(blocks, axis, split_axis=0, concat_axis=0, tiled=True)
    return arrived.sum(axis=0)


def sum_by_axis(x, axes, dim):
    far, near = axes
    blocks = in_blocks(x, dim, lax.axis_size(far))
    nearer = sum_at_owner(blocks, near, dim + 1)
    arrived = lax.all_to_all(nearer, far, split_axis=0, concat_axis=0, tiled=True)
    return arrived.sum(axis=0)


def total_of(x, axes):
    lines = x.reshape(-1, x.shape[-1])
    padded = filled_up(lines, lax.axis_size(axes[0]) * lax.axis_size(axes[1]))
    whole = whole_of(sum_by_axis(padded, axes, 0), axes, 0)
    return lax.slice_in_dim(whole, 0, len(lines)).reshape(x.shape)


def collect(x, axis, dim):
    blocks = copy_for_each(x, axis)
    return in_order(blocks, dim)


def total_of_2(x, axes):
    lines = x.reshape(-1, x.shape[-1])
    own = sum_at_owner(filled_up(lines, lax.axis_size(axes)), axes, 0)
    whole = collect(own, axes, 0)
    return whole[: len(lines)].reshape(x.shape)


def butterfly_sum(x, axes, masks):
    size = 1
    for a in axes:
        size *= lax.axis_size(a)
    for m in masks:
        x = x + lax.ppermute(x, axes, [(i, i ^ m) for i in range(size)])
    return x


def shifted(x, axis, s):
    n = lax.axis_size(axis)
    return lax.ppermute(x, axis, [(j, (j + s) % n) for j in range(n)])


def gather_rows(momentum, axis):
    n = lax.axis_size(axis)
    me = lax.axis_index(axis)
    mine = jnp.roll(momentum, -me, axis=0)
    pieces = [mine[0]] + [shifted(mine[s], axis, s) for s in range(1, n)]
    ordered = jnp.stack([pieces[(-i) % n] for i in range(n)])
    return jnp.roll(ordered, me, axis=0)


def scatter_rows(fresh, axis):
    n = lax.axis_size(axis)
    me = lax.axis_index(axis)
    mine = jnp.roll(fresh, -me, axis=0)
    pieces = [mine[0]] + [shifted(mine[s], axis, s) for s in range(1, n)]
    ordered = jnp.stack([pieces[(-i) % n] for i in range(n)])
    return jnp.roll(ordered, me, axis=0)


def inner_gram(columns):
    return lax.dot_general(
        columns, columns, (((0,), (0,)), ((), ())), precision=lax.Precision.HIGHEST
    )


def cholesky_pass(columns, gram_matrix):
    lower_factor = jnp.linalg.cholesky(gram_matrix)
    return lax.linalg.triangular_solve(
        lower_factor, columns, left_side=False, lower=True, transpose_a=True
    )


def shards(inputs, out_grads, test_matrix, momentum):
    features = inputs[0]
    errors = out_grads[0]
    probes = test_matrix[0]
    replicas = lax.axis_size(DP)
    scale = 1.0 / (features.shape[1] * features.shape[0] * replicas)
    projected = jnp.dot(features, probes, preferred_element_type=jnp.float32).astype(jnp.bfloat16)
    token_gram = lax.dot_general(
        errors, errors, (((1,), (1,)), ((), ())), preferred_element_type=jnp.float32
    ).astype(jnp.bfloat16)
    mixed_rows = jnp.dot(token_gram, projected, preferred_element_type=jnp.float32).astype(
        jnp.bfloat16
    )
    sketch_term = (
        lax.dot_general(
            features, mixed_rows, (((0,), (0,)), ((), ())), preferred_element_type=jnp.float32
        )
        * scale
    )
    sketch = total_of(sketch_term, (("dp_0", "dp_1"), "dp_2"))
    basis = cholesky_pass(sketch, inner_gram(sketch)).astype(jnp.bfloat16)
    reduced = jnp.dot(features, basis, preferred_element_type=jnp.float32).astype(jnp.bfloat16)
    shaped = jnp.dot(token_gram, reduced, preferred_element_type=jnp.float32).astype(jnp.bfloat16)
    core_term = (
        lax.dot_general(
            reduced, shaped, (((0,), (0,)), ((), ())), preferred_element_type=jnp.float32
        )
        * scale
    )
    core_matrix = butterfly_sum(core_term, DP, (1, 16, 2, 4, 8))
    shifted = core_matrix + jnp.eye(core_matrix.shape[0], dtype=jnp.float32)
    lower_factor = jnp.linalg.cholesky(shifted)
    half_solved = lax.linalg.triangular_solve(lower_factor, core_matrix, left_side=True, lower=True)
    factor = lax.linalg.triangular_solve(
        lower_factor, half_solved, left_side=True, lower=True, transpose_a=True
    )
    blocks = gather_rows(momentum, "blk")
    columns = blocks.reshape(-1, blocks.shape[-1])
    coeffs = lax.dot_general(
        basis, columns, (((0,), (0,)), ((), ())), preferred_element_type=jnp.float32
    )
    scaled = jnp.dot(factor, coeffs, precision=lax.Precision.HIGHEST).astype(jnp.bfloat16)
    fresh = (
        columns.astype(jnp.float32) - jnp.dot(basis, scaled, preferred_element_type=jnp.float32)
    ).astype(jnp.bfloat16)
    return scatter_rows(fresh.reshape(blocks.shape), "blk")


def solution(mesh):
    torus = Mesh(mesh.devices.reshape(2, 8, 2, mesh.shape["blk"]), ("dp_0", "dp_1", "dp_2", "blk"))
    in_specs = (P("blk", DP, None), P("blk", DP, None), P("blk", None, None), P(None, "blk", DP))
    out_specs = P(None, "blk", DP)
    return jax.shard_map(
        shards, mesh=torus, in_specs=in_specs, out_specs=out_specs, check_vma=False
    )
```

```python
import jax
import jax.numpy as jnp
from jax import lax
from jax.sharding import Mesh
from jax.sharding import PartitionSpec as P

DP = ("dp_0", "dp_1", "dp_2")


def filled_up(lines, devices):
    spare = -len(lines) % devices
    return jnp.pad(lines, [(0, spare)] + [(0, 0)] * (lines.ndim - 1))


def copy_for_each(x, axis):
    devices = lax.axis_size(axis)
    return lax.all_to_all(jnp.broadcast_to(x[None], (devices, *x.shape)), axis, 0, 0, tiled=True)


def in_order(blocks, dim):
    blocks = jnp.moveaxis(blocks, 0, dim)
    lengths = blocks.shape
    return blocks.reshape(*lengths[:dim], lengths[dim] * lengths[dim + 1], *lengths[dim + 2 :])


def whole_of(x, axes, dim):
    far, near = axes
    first = copy_for_each(x, far)
    blocks = jnp.swapaxes(copy_for_each(first, near), 0, 1)
    return in_order(blocks.reshape(-1, *x.shape), dim)


def in_blocks(x, dim, devices):
    lengths = x.shape
    blocks = x.reshape(*lengths[:dim], devices, lengths[dim] // devices, *lengths[dim + 1 :])
    return jnp.moveaxis(blocks, dim, 0)


def sum_at_owner(x, axis, dim):
    blocks = in_blocks(x, dim, lax.axis_size(axis))
    arrived = lax.all_to_all(blocks, axis, split_axis=0, concat_axis=0, tiled=True)
    return arrived.sum(axis=0)


def sum_by_axis(x, axes, dim):
    far, near = axes
    blocks = in_blocks(x, dim, lax.axis_size(far))
    nearer = sum_at_owner(blocks, near, dim + 1).astype(jnp.bfloat16)
    arrived = lax.all_to_all(nearer, far, split_axis=0, concat_axis=0, tiled=True)
    return arrived.astype(jnp.float32).sum(axis=0)


def total_of(x, axes):
    lines = x.reshape(-1, x.shape[-1])
    padded = filled_up(lines, lax.axis_size(axes[0]) * lax.axis_size(axes[1]))
    whole = whole_of(sum_by_axis(padded, axes, 0).astype(jnp.bfloat16), axes, 0)
    return lax.slice_in_dim(whole, 0, len(lines)).reshape(x.shape)


def collect(x, axis, dim):
    blocks = copy_for_each(x, axis)
    return in_order(blocks, dim)


def total_of_2(x, axes):
    lines = x.reshape(-1, x.shape[-1])
    own = sum_at_owner(filled_up(lines, lax.axis_size(axes)), axes, 0)
    whole = collect(own, axes, 0)
    return whole[: len(lines)].reshape(x.shape)


def butterfly_sum(x, axes, masks):
    size = 1
    for a in axes:
        size *= lax.axis_size(a)
    for m in masks:
        x = x + lax.ppermute(x, axes, [(i, i ^ m) for i in range(size)])
    return x


def shifted(x, axis, s):
    n = lax.axis_size(axis)
    return lax.ppermute(x, axis, [(j, (j + s) % n) for j in range(n)])


def gather_rows(momentum, axis):
    n = lax.axis_size(axis)
    me = lax.axis_index(axis)
    mine = jnp.roll(momentum, -me, axis=0)
    pieces = [mine[0]] + [shifted(mine[s], axis, s) for s in range(1, n)]
    ordered = jnp.stack([pieces[(-i) % n] for i in range(n)])
    return jnp.roll(ordered, me, axis=0)


def scatter_rows(fresh, axis):
    n = lax.axis_size(axis)
    me = lax.axis_index(axis)
    mine = jnp.roll(fresh, -me, axis=0)
    pieces = [mine[0]] + [shifted(mine[s], axis, s) for s in range(1, n)]
    ordered = jnp.stack([pieces[(-i) % n] for i in range(n)])
    return jnp.roll(ordered, me, axis=0)


def inner_gram(columns):
    return lax.dot_general(
        columns, columns, (((0,), (0,)), ((), ())), precision=lax.Precision.HIGHEST
    )


def cholesky_pass(columns, gram_matrix):
    lower_factor = jnp.linalg.cholesky(gram_matrix)
    return lax.linalg.triangular_solve(
        lower_factor, columns, left_side=False, lower=True, transpose_a=True
    )


def shards(inputs, out_grads, test_matrix, momentum):
    features = inputs[0]
    errors = out_grads[0]
    probes = test_matrix[0]
    replicas = lax.axis_size(DP)
    scale = 1.0 / (features.shape[1] * features.shape[0] * replicas)
    projected = jnp.dot(features, probes, preferred_element_type=jnp.float32).astype(jnp.bfloat16)
    token_gram = lax.dot_general(
        errors, errors, (((1,), (1,)), ((), ())), preferred_element_type=jnp.float32
    ).astype(jnp.bfloat16)
    mixed_rows = jnp.dot(token_gram, projected, preferred_element_type=jnp.float32).astype(
        jnp.bfloat16
    )
    sketch_term = (
        lax.dot_general(
            features, mixed_rows, (((0,), (0,)), ((), ())), preferred_element_type=jnp.float32
        )
        * scale
    )
    sketch = total_of(sketch_term, (("dp_0", "dp_1"), "dp_2")).astype(jnp.float32)
    basis = cholesky_pass(sketch, inner_gram(sketch)).astype(jnp.bfloat16)
    reduced = jnp.dot(features, basis, preferred_element_type=jnp.float32).astype(jnp.bfloat16)
    shaped = jnp.dot(token_gram, reduced, preferred_element_type=jnp.float32).astype(jnp.bfloat16)
    core_term = (
        lax.dot_general(
            reduced, shaped, (((0,), (0,)), ((), ())), preferred_element_type=jnp.float32
        )
        * scale
    )
    core_matrix = butterfly_sum(core_term, DP, (1, 16, 2, 4, 8))
    shifted = core_matrix + jnp.eye(core_matrix.shape[0], dtype=jnp.float32)
    lower_factor = jnp.linalg.cholesky(shifted)
    half_solved = lax.linalg.triangular_solve(lower_factor, core_matrix, left_side=True, lower=True)
    factor = lax.linalg.triangular_solve(
        lower_factor, half_solved, left_side=True, lower=True, transpose_a=True
    )
    blocks = gather_rows(momentum, "blk")
    columns = blocks.reshape(-1, blocks.shape[-1])
    coeffs = lax.dot_general(
        basis, columns, (((0,), (0,)), ((), ())), preferred_element_type=jnp.float32
    )
    scaled = jnp.dot(factor, coeffs, precision=lax.Precision.HIGHEST).astype(jnp.bfloat16)
    fresh = (
        columns.astype(jnp.float32) - jnp.dot(basis, scaled, preferred_element_type=jnp.float32)
    ).astype(jnp.bfloat16)
    return scatter_rows(fresh.reshape(blocks.shape), "blk")


def solution(mesh):
    torus = Mesh(mesh.devices.reshape(2, 8, 2, mesh.shape["blk"]), ("dp_0", "dp_1", "dp_2", "blk"))
    in_specs = (P("blk", DP, None), P("blk", DP, None), P("blk", None, None), P(None, "blk", DP))
    out_specs = P(None, "blk", DP)
    return jax.shard_map(
        shards, mesh=torus, in_specs=in_specs, out_specs=out_specs, check_vma=False
    )
```

```python
import jax
import jax.numpy as jnp
from jax import lax
from jax.sharding import Mesh
from jax.sharding import PartitionSpec as P

DP = ("dp_0", "dp_1", "dp_2")


def filled_up(lines, devices):
    spare = -len(lines) % devices
    return jnp.pad(lines, [(0, spare)] + [(0, 0)] * (lines.ndim - 1))


def copy_for_each(x, axis):
    devices = lax.axis_size(axis)
    return lax.all_to_all(jnp.broadcast_to(x[None], (devices, *x.shape)), axis, 0, 0, tiled=True)


def in_order(blocks, dim):
    blocks = jnp.moveaxis(blocks, 0, dim)
    lengths = blocks.shape
    return blocks.reshape(*lengths[:dim], lengths[dim] * lengths[dim + 1], *lengths[dim + 2 :])


def whole_of(x, axes, dim):
    far, near = axes
    first = copy_for_each(x, far)
    blocks = jnp.swapaxes(copy_for_each(first, near), 0, 1)
    return in_order(blocks.reshape(-1, *x.shape), dim)


def in_blocks(x, dim, devices):
    lengths = x.shape
    blocks = x.reshape(*lengths[:dim], devices, lengths[dim] // devices, *lengths[dim + 1 :])
    return jnp.moveaxis(blocks, dim, 0)


def sum_at_owner(x, axis, dim):
    blocks = in_blocks(x, dim, lax.axis_size(axis))
    arrived = lax.all_to_all(blocks, axis, split_axis=0, concat_axis=0, tiled=True)
    return arrived.sum(axis=0)


def sum_by_axis(x, axes, dim):
    far, near = axes
    blocks = in_blocks(x, dim, lax.axis_size(far))
    nearer = sum_at_owner(blocks, near, dim + 1).astype(jnp.bfloat16)
    arrived = lax.all_to_all(nearer, far, split_axis=0, concat_axis=0, tiled=True)
    return arrived.astype(jnp.float32).sum(axis=0)


def total_of(x, axes):
    lines = x.reshape(-1, x.shape[-1])
    padded = filled_up(lines, lax.axis_size(axes[0]) * lax.axis_size(axes[1]))
    whole = whole_of(sum_by_axis(padded, axes, 0).astype(jnp.bfloat16), axes, 0)
    return lax.slice_in_dim(whole, 0, len(lines)).reshape(x.shape)


def collect(x, axis, dim):
    blocks = copy_for_each(x, axis)
    return in_order(blocks, dim)


def total_of_2(x, axes):
    lines = x.reshape(-1, x.shape[-1])
    own = sum_at_owner(filled_up(lines, lax.axis_size(axes)), axes, 0)
    whole = collect(own, axes, 0)
    return whole[: len(lines)].reshape(x.shape)


def butterfly_sum(x, axes, masks):
    size = 1
    for a in axes:
        size *= lax.axis_size(a)
    for m in masks:
        x = x + lax.ppermute(x, axes, [(i, i ^ m) for i in range(size)])
    return x


def shifted(x, axis, s):
    n = lax.axis_size(axis)
    return lax.ppermute(x, axis, [(j, (j + s) % n) for j in range(n)])


def gather_rows(momentum, axis):
    n = lax.axis_size(axis)
    me = lax.axis_index(axis)
    mine = jnp.roll(momentum, -me, axis=0)
    pieces = [mine[0]] + [shifted(mine[s], axis, s) for s in range(1, n)]
    ordered = jnp.stack([pieces[(-i) % n] for i in range(n)])
    return jnp.roll(ordered, me, axis=0)


def scatter_rows(fresh, axis):
    n = lax.axis_size(axis)
    me = lax.axis_index(axis)
    mine = jnp.roll(fresh, -me, axis=0)
    pieces = [mine[0]] + [shifted(mine[s], axis, s) for s in range(1, n)]
    ordered = jnp.stack([pieces[(-i) % n] for i in range(n)])
    return jnp.roll(ordered, me, axis=0)


def inner_gram(columns):
    return lax.dot_general(
        columns, columns, (((0,), (0,)), ((), ())), precision=lax.Precision.HIGHEST
    )


def mm(a, b):
    return jnp.dot(a, b, precision=lax.Precision.HIGHEST)


def inverse_factor(matrix):
    half = matrix.shape[0] // 2
    sym = (matrix + matrix.T) * 0.5
    eye = jnp.eye(half, dtype=jnp.float32)
    l11 = lax.linalg.cholesky(sym[:half, :half], symmetrize_input=False)
    i11 = lax.linalg.triangular_solve(l11, eye, left_side=True, lower=True)
    l21 = mm(sym[half:, :half], i11.T)
    rest = sym[half:, half:] - mm(l21, l21.T)
    l22 = lax.linalg.cholesky(rest, symmetrize_input=True)
    i22 = lax.linalg.triangular_solve(l22, eye, left_side=True, lower=True)
    i21 = -mm(i22, mm(l21, i11))
    top = jnp.concatenate([i11, jnp.zeros_like(i11)], axis=1)
    bottom = jnp.concatenate([i21, i22], axis=1)
    return jnp.concatenate([top, bottom], axis=0)


def cholesky_pass(columns, gram_matrix):
    return mm(columns, inverse_factor(gram_matrix).T)


def shards(inputs, out_grads, test_matrix, momentum):
    features = inputs[0]
    errors = out_grads[0]
    probes = test_matrix[0]
    replicas = lax.axis_size(DP)
    scale = 1.0 / (features.shape[1] * features.shape[0] * replicas)
    projected = jnp.dot(features, probes, preferred_element_type=jnp.float32).astype(jnp.bfloat16)
    token_gram = lax.dot_general(
        errors, errors, (((1,), (1,)), ((), ())), preferred_element_type=jnp.float32
    ).astype(jnp.bfloat16)
    mixed_rows = jnp.dot(token_gram, projected, preferred_element_type=jnp.float32).astype(
        jnp.bfloat16
    )
    sketch_term = (
        lax.dot_general(
            features, mixed_rows, (((0,), (0,)), ((), ())), preferred_element_type=jnp.float32
        )
        * scale
    )
    sketch = total_of(sketch_term, (("dp_0", "dp_1"), "dp_2")).astype(jnp.float32)
    basis = cholesky_pass(sketch, inner_gram(sketch)).astype(jnp.bfloat16)
    reduced = jnp.dot(features, basis, preferred_element_type=jnp.float32).astype(jnp.bfloat16)
    shaped = jnp.dot(token_gram, reduced, preferred_element_type=jnp.float32).astype(jnp.bfloat16)
    core_term = (
        lax.dot_general(
            reduced, shaped, (((0,), (0,)), ((), ())), preferred_element_type=jnp.float32
        )
        * scale
    )
    core_matrix = butterfly_sum(core_term, DP, (1, 16, 2, 4, 8))
    shifted = core_matrix + jnp.eye(core_matrix.shape[0], dtype=jnp.float32)
    inverse = inverse_factor(shifted)
    factor = mm(inverse.T, mm(inverse, core_matrix))
    blocks = gather_rows(momentum, "blk")
    columns = blocks.reshape(-1, blocks.shape[-1])
    coeffs = lax.dot_general(
        basis, columns, (((0,), (0,)), ((), ())), preferred_element_type=jnp.float32
    )
    scaled = jnp.dot(factor, coeffs, precision=lax.Precision.HIGHEST).astype(jnp.bfloat16)
    fresh = (
        columns.astype(jnp.float32) - jnp.dot(basis, scaled, preferred_element_type=jnp.float32)
    ).astype(jnp.bfloat16)
    return scatter_rows(fresh.reshape(blocks.shape), "blk")


def solution(mesh):
    torus = Mesh(mesh.devices.reshape(2, 8, 2, mesh.shape["blk"]), ("dp_0", "dp_1", "dp_2", "blk"))
    in_specs = (P("blk", DP, None), P("blk", DP, None), P("blk", None, None), P(None, "blk", DP))
    out_specs = P(None, "blk", DP)
    return jax.shard_map(
        shards, mesh=torus, in_specs=in_specs, out_specs=out_specs, check_vma=False
    )
```

```python
import jax
import jax.numpy as jnp
from jax import lax
from jax.sharding import Mesh
from jax.sharding import PartitionSpec as P

DP = ("dp_0", "dp_1", "dp_2")


def filled_up(lines, devices):
    spare = -len(lines) % devices
    return jnp.pad(lines, [(0, spare)] + [(0, 0)] * (lines.ndim - 1))


def copy_for_each(x, axis):
    devices = lax.axis_size(axis)
    return lax.all_to_all(jnp.broadcast_to(x[None], (devices, *x.shape)), axis, 0, 0, tiled=True)


def in_order(blocks, dim):
    blocks = jnp.moveaxis(blocks, 0, dim)
    lengths = blocks.shape
    return blocks.reshape(*lengths[:dim], lengths[dim] * lengths[dim + 1], *lengths[dim + 2 :])


def whole_of(x, axes, dim):
    far, near = axes
    first = copy_for_each(x, far)
    blocks = jnp.swapaxes(copy_for_each(first, near), 0, 1)
    return in_order(blocks.reshape(-1, *x.shape), dim)


def in_blocks(x, dim, devices):
    lengths = x.shape
    blocks = x.reshape(*lengths[:dim], devices, lengths[dim] // devices, *lengths[dim + 1 :])
    return jnp.moveaxis(blocks, dim, 0)


def sum_at_owner(x, axis, dim):
    blocks = in_blocks(x, dim, lax.axis_size(axis))
    arrived = lax.all_to_all(blocks, axis, split_axis=0, concat_axis=0, tiled=True)
    return arrived.sum(axis=0)


def sum_by_axis(x, axes, dim):
    far, near = axes
    blocks = in_blocks(x, dim, lax.axis_size(far))
    nearer = sum_at_owner(blocks, near, dim + 1).astype(jnp.bfloat16)
    arrived = lax.all_to_all(nearer, far, split_axis=0, concat_axis=0, tiled=True)
    return arrived.astype(jnp.float32).sum(axis=0)


def total_of(x, axes):
    lines = x.reshape(-1, x.shape[-1])
    padded = filled_up(lines, lax.axis_size(axes[0]) * lax.axis_size(axes[1]))
    whole = whole_of(sum_by_axis(padded, axes, 0).astype(jnp.bfloat16), axes, 0)
    return lax.slice_in_dim(whole, 0, len(lines)).reshape(x.shape)


def collect(x, axis, dim):
    blocks = copy_for_each(x, axis)
    return in_order(blocks, dim)


def total_of_2(x, axes):
    lines = x.reshape(-1, x.shape[-1])
    own = sum_at_owner(filled_up(lines, lax.axis_size(axes)), axes, 0)
    whole = collect(own, axes, 0)
    return whole[: len(lines)].reshape(x.shape)


def butterfly_sum(x, axes, masks):
    size = 1
    for a in axes:
        size *= lax.axis_size(a)
    for m in masks:
        x = x + lax.ppermute(x, axes, [(i, i ^ m) for i in range(size)])
    return x


def shifted(x, axis, s):
    n = lax.axis_size(axis)
    return lax.ppermute(x, axis, [(j, (j + s) % n) for j in range(n)])


def spread(stack, axis):
    n = lax.axis_size(axis)
    me = lax.axis_index(axis)
    mine = jnp.roll(stack, -me, axis=0)
    pieces = [mine[0]] + [shifted(mine[s], axis, s) for s in range(1, n)]
    ordered = jnp.stack([pieces[(-i) % n] for i in range(n)])
    return jnp.roll(ordered, me, axis=0)


def gather_all(x, axis):
    n = lax.axis_size(axis)
    me = lax.axis_index(axis)
    pieces = [x] + [shifted(x, axis, s) for s in range(1, n)]
    ordered = jnp.stack([pieces[(-i) % n] for i in range(n)])
    return jnp.roll(ordered, me, axis=0)


def ring_sum(x, axis):
    n = lax.axis_size(axis)
    own = spread(x.reshape(n, x.shape[0] // n, *x.shape[1:]), axis).sum(axis=0)
    return gather_all(own, axis).reshape(x.shape)


def inner_gram(columns):
    return lax.dot_general(
        columns, columns, (((0,), (0,)), ((), ())), precision=lax.Precision.HIGHEST
    )


def mm(a, b):
    return jnp.dot(a, b, precision=lax.Precision.HIGHEST)


def inverse_factor(matrix):
    half = matrix.shape[0] // 2
    sym = (matrix + matrix.T) * 0.5
    eye = jnp.eye(half, dtype=jnp.float32)
    l11 = lax.linalg.cholesky(sym[:half, :half], symmetrize_input=False)
    i11 = lax.linalg.triangular_solve(l11, eye, left_side=True, lower=True)
    l21 = mm(sym[half:, :half], i11.T)
    rest = sym[half:, half:] - mm(l21, l21.T)
    l22 = lax.linalg.cholesky(rest, symmetrize_input=True)
    i22 = lax.linalg.triangular_solve(l22, eye, left_side=True, lower=True)
    i21 = -mm(i22, mm(l21, i11))
    top = jnp.concatenate([i11, jnp.zeros_like(i11)], axis=1)
    bottom = jnp.concatenate([i21, i22], axis=1)
    return jnp.concatenate([top, bottom], axis=0)


def cholesky_pass(columns, gram_matrix):
    return mm(columns, inverse_factor(gram_matrix).T)


def shards(inputs, out_grads, test_matrix, momentum):
    features = inputs[0]
    errors = out_grads[0]
    probes = test_matrix[0]
    replicas = lax.axis_size(DP)
    scale = 1.0 / (features.shape[1] * features.shape[0] * replicas)
    projected = jnp.dot(features, probes, preferred_element_type=jnp.float32).astype(jnp.bfloat16)
    token_gram = lax.dot_general(
        errors, errors, (((1,), (1,)), ((), ())), preferred_element_type=jnp.float32
    ).astype(jnp.bfloat16)
    mixed_rows = jnp.dot(token_gram, projected, preferred_element_type=jnp.float32).astype(
        jnp.bfloat16
    )
    sketch_term = (
        lax.dot_general(
            features, mixed_rows, (((0,), (0,)), ((), ())), preferred_element_type=jnp.float32
        )
        * scale
    )
    sketch = total_of(sketch_term, (("dp_0", "dp_1"), "dp_2")).astype(jnp.float32)
    basis = cholesky_pass(sketch, inner_gram(sketch)).astype(jnp.bfloat16)
    reduced = jnp.dot(features, basis, preferred_element_type=jnp.float32).astype(jnp.bfloat16)
    shaped = jnp.dot(token_gram, reduced, preferred_element_type=jnp.float32).astype(jnp.bfloat16)
    core_term = (
        lax.dot_general(
            reduced, shaped, (((0,), (0,)), ((), ())), preferred_element_type=jnp.float32
        )
        * scale
    )
    core_matrix = ring_sum(butterfly_sum(core_term, DP, (1, 16)), "dp_1")
    shifted = core_matrix + jnp.eye(core_matrix.shape[0], dtype=jnp.float32)
    inverse = inverse_factor(shifted)
    factor = mm(inverse.T, mm(inverse, core_matrix))
    blocks = spread(momentum, "blk")
    columns = blocks.reshape(-1, blocks.shape[-1])
    coeffs = lax.dot_general(
        basis, columns, (((0,), (0,)), ((), ())), preferred_element_type=jnp.float32
    )
    scaled = jnp.dot(factor, coeffs, precision=lax.Precision.HIGHEST).astype(jnp.bfloat16)
    fresh = (
        columns.astype(jnp.float32) - jnp.dot(basis, scaled, preferred_element_type=jnp.float32)
    ).astype(jnp.bfloat16)
    return spread(fresh.reshape(blocks.shape), "blk")


def solution(mesh):
    torus = Mesh(mesh.devices.reshape(2, 8, 2, mesh.shape["blk"]), ("dp_0", "dp_1", "dp_2", "blk"))
    in_specs = (P("blk", DP, None), P("blk", DP, None), P("blk", None, None), P(None, "blk", DP))
    out_specs = P(None, "blk", DP)
    return jax.shard_map(
        shards, mesh=torus, in_specs=in_specs, out_specs=out_specs, check_vma=False
    )
```

```python
import jax
import jax.numpy as jnp
from jax import lax
from jax.sharding import Mesh
from jax.sharding import PartitionSpec as P

DP = ("dp_0", "dp_1", "dp_2")


def filled_up(lines, devices):
    spare = -len(lines) % devices
    return jnp.pad(lines, [(0, spare)] + [(0, 0)] * (lines.ndim - 1))


def copy_for_each(x, axis):
    devices = lax.axis_size(axis)
    return lax.all_to_all(jnp.broadcast_to(x[None], (devices, *x.shape)), axis, 0, 0, tiled=True)


def in_order(blocks, dim):
    blocks = jnp.moveaxis(blocks, 0, dim)
    lengths = blocks.shape
    return blocks.reshape(*lengths[:dim], lengths[dim] * lengths[dim + 1], *lengths[dim + 2 :])


def whole_of(x, axes, dim):
    far, near = axes
    first = copy_for_each(x, far)
    blocks = jnp.swapaxes(copy_for_each(first, near), 0, 1)
    return in_order(blocks.reshape(-1, *x.shape), dim)


def in_blocks(x, dim, devices):
    lengths = x.shape
    blocks = x.reshape(*lengths[:dim], devices, lengths[dim] // devices, *lengths[dim + 1 :])
    return jnp.moveaxis(blocks, dim, 0)


def sum_at_owner(x, axis, dim):
    blocks = in_blocks(x, dim, lax.axis_size(axis))
    arrived = lax.all_to_all(blocks, axis, split_axis=0, concat_axis=0, tiled=True)
    return arrived.sum(axis=0)


def sum_by_axis(x, axes, dim):
    far, near = axes
    blocks = in_blocks(x, dim, lax.axis_size(far))
    nearer = sum_at_owner(blocks, near, dim + 1).astype(jnp.bfloat16)
    arrived = lax.all_to_all(nearer, far, split_axis=0, concat_axis=0, tiled=True)
    return arrived.astype(jnp.float32).sum(axis=0)


def total_of(x, axes):
    lines = x.reshape(-1, x.shape[-1])
    padded = filled_up(lines, lax.axis_size(axes[0]) * lax.axis_size(axes[1]))
    whole = whole_of(sum_by_axis(padded, axes, 0).astype(jnp.bfloat16), axes, 0)
    return lax.slice_in_dim(whole, 0, len(lines)).reshape(x.shape)


def collect(x, axis, dim):
    blocks = copy_for_each(x, axis)
    return in_order(blocks, dim)


def total_of_2(x, axes):
    lines = x.reshape(-1, x.shape[-1])
    own = sum_at_owner(filled_up(lines, lax.axis_size(axes)), axes, 0)
    whole = collect(own, axes, 0)
    return whole[: len(lines)].reshape(x.shape)


def butterfly_sum(x, axes, masks):
    size = 1
    for a in axes:
        size *= lax.axis_size(a)
    for m in masks:
        x = x + lax.ppermute(x, axes, [(i, i ^ m) for i in range(size)])
    return x


def shifted(x, axis, s):
    n = lax.axis_size(axis)
    return lax.ppermute(x, axis, [(j, (j + s) % n) for j in range(n)])


def spread(stack, axis):
    n = lax.axis_size(axis)
    me = lax.axis_index(axis)
    mine = jnp.roll(stack, -me, axis=0)
    pieces = [mine[0]] + [shifted(mine[s], axis, s) for s in range(1, n)]
    ordered = jnp.stack([pieces[(-i) % n] for i in range(n)])
    return jnp.roll(ordered, me, axis=0)


def gather_all(x, axis):
    n = lax.axis_size(axis)
    me = lax.axis_index(axis)
    pieces = [x] + [shifted(x, axis, s) for s in range(1, n)]
    ordered = jnp.stack([pieces[(-i) % n] for i in range(n)])
    return jnp.roll(ordered, me, axis=0)


def ring_sum(x, axis):
    n = lax.axis_size(axis)
    parts = x.reshape(n, x.shape[0] // n, *x.shape[1:])
    own = lax.all_to_all(parts, axis, 0, 0, tiled=True).sum(axis=0)
    return collect(own, axis, 0)


def inner_gram(columns):
    return lax.dot_general(
        columns, columns, (((0,), (0,)), ((), ())), precision=lax.Precision.HIGHEST
    )


def mm(a, b):
    return jnp.dot(a, b, precision=lax.Precision.HIGHEST)


def inverse_factor(matrix):
    half = matrix.shape[0] // 2
    sym = (matrix + matrix.T) * 0.5
    eye = jnp.eye(half, dtype=jnp.float32)
    l11 = lax.linalg.cholesky(sym[:half, :half], symmetrize_input=False)
    i11 = lax.linalg.triangular_solve(l11, eye, left_side=True, lower=True)
    l21 = mm(sym[half:, :half], i11.T)
    rest = sym[half:, half:] - mm(l21, l21.T)
    l22 = lax.linalg.cholesky(rest, symmetrize_input=True)
    i22 = lax.linalg.triangular_solve(l22, eye, left_side=True, lower=True)
    i21 = -mm(i22, mm(l21, i11))
    top = jnp.concatenate([i11, jnp.zeros_like(i11)], axis=1)
    bottom = jnp.concatenate([i21, i22], axis=1)
    return jnp.concatenate([top, bottom], axis=0)


def cholesky_pass(columns, gram_matrix):
    return mm(columns, inverse_factor(gram_matrix).T)


def shards(inputs, out_grads, test_matrix, momentum):
    features = inputs[0]
    errors = out_grads[0]
    probes = test_matrix[0]
    replicas = lax.axis_size(DP)
    scale = 1.0 / (features.shape[1] * features.shape[0] * replicas)
    projected = jnp.dot(features, probes, preferred_element_type=jnp.float32).astype(jnp.bfloat16)
    token_gram = lax.dot_general(
        errors, errors, (((1,), (1,)), ((), ())), preferred_element_type=jnp.float32
    ).astype(jnp.bfloat16)
    mixed_rows = jnp.dot(token_gram, projected, preferred_element_type=jnp.float32).astype(
        jnp.bfloat16
    )
    sketch_term = (
        lax.dot_general(
            features, mixed_rows, (((0,), (0,)), ((), ())), preferred_element_type=jnp.float32
        )
        * scale
    )
    sketch = total_of(sketch_term, (("dp_0", "dp_1"), "dp_2")).astype(jnp.float32)
    basis = cholesky_pass(sketch, inner_gram(sketch)).astype(jnp.bfloat16)
    reduced = jnp.dot(features, basis, preferred_element_type=jnp.float32).astype(jnp.bfloat16)
    shaped = jnp.dot(token_gram, reduced, preferred_element_type=jnp.float32).astype(jnp.bfloat16)
    core_term = (
        lax.dot_general(
            reduced, shaped, (((0,), (0,)), ((), ())), preferred_element_type=jnp.float32
        )
        * scale
    )
    core_matrix = ring_sum(butterfly_sum(core_term, DP, (1, 16)), "dp_1")
    shifted = core_matrix + jnp.eye(core_matrix.shape[0], dtype=jnp.float32)
    inverse = inverse_factor(shifted)
    factor = mm(inverse.T, mm(inverse, core_matrix))
    blocks = spread(momentum, "blk")
    columns = blocks.reshape(-1, blocks.shape[-1])
    coeffs = lax.dot_general(
        basis, columns, (((0,), (0,)), ((), ())), preferred_element_type=jnp.float32
    )
    scaled = jnp.dot(factor, coeffs, precision=lax.Precision.HIGHEST).astype(jnp.bfloat16)
    fresh = (
        columns.astype(jnp.float32) - jnp.dot(basis, scaled, preferred_element_type=jnp.float32)
    ).astype(jnp.bfloat16)
    return spread(fresh.reshape(blocks.shape), "blk")


def solution(mesh):
    torus = Mesh(mesh.devices.reshape(2, 8, 2, mesh.shape["blk"]), ("dp_0", "dp_1", "dp_2", "blk"))
    in_specs = (P("blk", DP, None), P("blk", DP, None), P("blk", None, None), P(None, "blk", DP))
    out_specs = P(None, "blk", DP)
    return jax.shard_map(
        shards, mesh=torus, in_specs=in_specs, out_specs=out_specs, check_vma=False
    )
```

```python
import jax
import jax.numpy as jnp
from jax import lax
from jax.sharding import Mesh
from jax.sharding import PartitionSpec as P

DP = ("dp_0", "dp_1", "dp_2")


def filled_up(lines, devices):
    spare = -len(lines) % devices
    return jnp.pad(lines, [(0, spare)] + [(0, 0)] * (lines.ndim - 1))


def copy_for_each(x, axis):
    devices = lax.axis_size(axis)
    return lax.all_to_all(jnp.broadcast_to(x[None], (devices, *x.shape)), axis, 0, 0, tiled=True)


def in_order(blocks, dim):
    blocks = jnp.moveaxis(blocks, 0, dim)
    lengths = blocks.shape
    return blocks.reshape(*lengths[:dim], lengths[dim] * lengths[dim + 1], *lengths[dim + 2 :])


def whole_of(x, axes, dim):
    far, near = axes
    first = copy_for_each(x, far)
    blocks = jnp.swapaxes(copy_for_each(first, near), 0, 1)
    return in_order(blocks.reshape(-1, *x.shape), dim)


def in_blocks(x, dim, devices):
    lengths = x.shape
    blocks = x.reshape(*lengths[:dim], devices, lengths[dim] // devices, *lengths[dim + 1 :])
    return jnp.moveaxis(blocks, dim, 0)


def sum_at_owner(x, axis, dim):
    blocks = in_blocks(x, dim, lax.axis_size(axis))
    arrived = lax.all_to_all(blocks, axis, split_axis=0, concat_axis=0, tiled=True)
    return arrived.sum(axis=0)


def sum_by_axis(x, axes, dim):
    far, near = axes
    blocks = in_blocks(x, dim, lax.axis_size(far))
    nearer = sum_at_owner(blocks, near, dim + 1).astype(jnp.bfloat16)
    arrived = lax.all_to_all(nearer, far, split_axis=0, concat_axis=0, tiled=True)
    return arrived.astype(jnp.float32).sum(axis=0)


def total_of(x, axes):
    lines = x.reshape(-1, x.shape[-1])
    padded = filled_up(lines, lax.axis_size(axes[0]) * lax.axis_size(axes[1]))
    whole = whole_of(sum_by_axis(padded, axes, 0).astype(jnp.bfloat16), axes, 0)
    return lax.slice_in_dim(whole, 0, len(lines)).reshape(x.shape)


def collect(x, axis, dim):
    blocks = copy_for_each(x, axis)
    return in_order(blocks, dim)


def total_of_2(x, axes):
    lines = x.reshape(-1, x.shape[-1])
    own = sum_at_owner(filled_up(lines, lax.axis_size(axes)), axes, 0)
    whole = collect(own, axes, 0)
    return whole[: len(lines)].reshape(x.shape)


def butterfly_sum(x, axes, masks):
    size = 1
    for a in axes:
        size *= lax.axis_size(a)
    for m in masks:
        x = x + lax.ppermute(x, axes, [(i, i ^ m) for i in range(size)])
    return x


def shifted(x, axis, s):
    n = lax.axis_size(axis)
    return lax.ppermute(x, axis, [(j, (j + s) % n) for j in range(n)])


def spread(stack, axis):
    n = lax.axis_size(axis)
    me = lax.axis_index(axis)
    mine = jnp.roll(stack, -me, axis=0)
    pieces = [mine[0]] + [shifted(mine[s], axis, s) for s in range(1, n)]
    ordered = jnp.stack([pieces[(-i) % n] for i in range(n)])
    return jnp.roll(ordered, me, axis=0)


def gather_all(x, axis):
    n = lax.axis_size(axis)
    me = lax.axis_index(axis)
    pieces = [x] + [shifted(x, axis, s) for s in range(1, n)]
    ordered = jnp.stack([pieces[(-i) % n] for i in range(n)])
    return jnp.roll(ordered, me, axis=0)


def ring_sum(x, axis):
    n = lax.axis_size(axis)
    parts = x.reshape(n, x.shape[0] // n, *x.shape[1:])
    own = lax.all_to_all(parts, axis, 0, 0, tiled=True).sum(axis=0)
    return collect(own, axis, 0)


def inner_gram(columns):
    return lax.dot_general(
        columns, columns, (((0,), (0,)), ((), ())), precision=lax.Precision.HIGHEST
    )


def mm(a, b):
    return jnp.dot(a, b, precision=lax.Precision.HIGHEST)


def inverse_factor(matrix):
    half = matrix.shape[0] // 2
    sym = (matrix + matrix.T) * 0.5
    eye = jnp.eye(half, dtype=jnp.float32)
    l11 = lax.linalg.cholesky(sym[:half, :half], symmetrize_input=False)
    i11 = lax.linalg.triangular_solve(l11, eye, left_side=True, lower=True)
    l21 = mm(sym[half:, :half], i11.T)
    rest = sym[half:, half:] - mm(l21, l21.T)
    l22 = lax.linalg.cholesky(rest, symmetrize_input=True)
    i22 = lax.linalg.triangular_solve(l22, eye, left_side=True, lower=True)
    i21 = -mm(i22, mm(l21, i11))
    top = jnp.concatenate([i11, jnp.zeros_like(i11)], axis=1)
    bottom = jnp.concatenate([i21, i22], axis=1)
    return jnp.concatenate([top, bottom], axis=0)


def cholesky_pass(columns, gram_matrix):
    return mm(columns, inverse_factor(gram_matrix).T)


def shards(inputs, out_grads, test_matrix, momentum):
    features = inputs[0]
    errors = out_grads[0]
    probes = test_matrix[0]
    replicas = lax.axis_size(DP)
    scale = 1.0 / (features.shape[1] * features.shape[0] * replicas)
    projected = jnp.dot(features, probes, preferred_element_type=jnp.float32).astype(jnp.bfloat16)
    token_gram = lax.dot_general(
        errors, errors, (((1,), (1,)), ((), ())), preferred_element_type=jnp.float32
    ).astype(jnp.bfloat16)
    mixed_rows = jnp.dot(token_gram, projected, preferred_element_type=jnp.float32).astype(
        jnp.bfloat16
    )
    sketch_term = (
        lax.dot_general(
            features, mixed_rows, (((0,), (0,)), ((), ())), preferred_element_type=jnp.float32
        )
        * scale
    )
    sketch = total_of(sketch_term, (("dp_0", "dp_1"), "dp_2")).astype(jnp.float32)
    basis = cholesky_pass(sketch, inner_gram(sketch)).astype(jnp.bfloat16)
    reduced = jnp.dot(features, basis, preferred_element_type=jnp.float32).astype(jnp.bfloat16)
    shaped = jnp.dot(token_gram, reduced, preferred_element_type=jnp.float32).astype(jnp.bfloat16)
    core_term = (
        lax.dot_general(
            reduced, shaped, (((0,), (0,)), ((), ())), preferred_element_type=jnp.float32
        )
        * scale
    )
    core_matrix = ring_sum(butterfly_sum(core_term, DP, (1, 16)), "dp_1")
    shifted = core_matrix + jnp.eye(core_matrix.shape[0], dtype=jnp.float32)
    inverse = inverse_factor(shifted)
    factor = mm(inverse.T, mm(inverse, core_matrix))
    columns = lax.all_to_all(momentum, "blk", split_axis=0, concat_axis=1, tiled=True)[0]
    coeffs = lax.dot_general(
        basis, columns, (((0,), (0,)), ((), ())), preferred_element_type=jnp.float32
    )
    scaled = jnp.dot(factor, coeffs, precision=lax.Precision.HIGHEST).astype(jnp.bfloat16)
    fresh = (
        columns.astype(jnp.float32) - jnp.dot(basis, scaled, preferred_element_type=jnp.float32)
    ).astype(jnp.bfloat16)
    return spread(fresh.reshape(momentum.shape), "blk")


def solution(mesh):
    torus = Mesh(mesh.devices.reshape(2, 8, 2, mesh.shape["blk"]), ("dp_0", "dp_1", "dp_2", "blk"))
    in_specs = (P("blk", DP, None), P("blk", DP, None), P("blk", None, None), P(None, "blk", DP))
    out_specs = P(None, "blk", DP)
    return jax.shard_map(
        shards, mesh=torus, in_specs=in_specs, out_specs=out_specs, check_vma=False
    )
```

```python
import functools
import jax
import jax.numpy as jnp
from jax import lax
from jax.sharding import Mesh
from jax.sharding import PartitionSpec as P
from jax.experimental import pallas as pl
from jax.experimental.pallas import tpu as pltpu

DP = ("dp_0", "dp_1", "dp_2")


def filled_up(lines, devices):
    spare = -len(lines) % devices
    return jnp.pad(lines, [(0, spare)] + [(0, 0)] * (lines.ndim - 1))


def copy_for_each(x, axis):
    devices = lax.axis_size(axis)
    return lax.all_to_all(jnp.broadcast_to(x[None], (devices, *x.shape)), axis, 0, 0, tiled=True)


def in_order(blocks, dim):
    blocks = jnp.moveaxis(blocks, 0, dim)
    lengths = blocks.shape
    return blocks.reshape(*lengths[:dim], lengths[dim] * lengths[dim + 1], *lengths[dim + 2 :])


def whole_of(x, axes, dim):
    far, near = axes
    first = copy_for_each(x, far)
    blocks = jnp.swapaxes(copy_for_each(first, near), 0, 1)
    return in_order(blocks.reshape(-1, *x.shape), dim)


def in_blocks(x, dim, devices):
    lengths = x.shape
    blocks = x.reshape(*lengths[:dim], devices, lengths[dim] // devices, *lengths[dim + 1 :])
    return jnp.moveaxis(blocks, dim, 0)


def sum_at_owner(x, axis, dim):
    blocks = in_blocks(x, dim, lax.axis_size(axis))
    arrived = lax.all_to_all(blocks, axis, split_axis=0, concat_axis=0, tiled=True)
    return arrived.sum(axis=0)


def sum_by_axis(x, axes, dim):
    far, near = axes
    blocks = in_blocks(x, dim, lax.axis_size(far))
    nearer = sum_at_owner(blocks, near, dim + 1).astype(jnp.bfloat16)
    arrived = lax.all_to_all(nearer, far, split_axis=0, concat_axis=0, tiled=True)
    return arrived.astype(jnp.float32).sum(axis=0)


def total_of(x, axes):
    lines = x.reshape(-1, x.shape[-1])
    padded = filled_up(lines, lax.axis_size(axes[0]) * lax.axis_size(axes[1]))
    whole = whole_of(sum_by_axis(padded, axes, 0).astype(jnp.bfloat16), axes, 0)
    return lax.slice_in_dim(whole, 0, len(lines)).reshape(x.shape)


def collect(x, axis, dim):
    blocks = copy_for_each(x, axis)
    return in_order(blocks, dim)


def total_of_2(x, axes):
    lines = x.reshape(-1, x.shape[-1])
    own = sum_at_owner(filled_up(lines, lax.axis_size(axes)), axes, 0)
    whole = collect(own, axes, 0)
    return whole[: len(lines)].reshape(x.shape)


def butterfly_sum(x, axes, masks):
    size = 1
    for a in axes:
        size *= lax.axis_size(a)
    for m in masks:
        x = x + lax.ppermute(x, axes, [(i, i ^ m) for i in range(size)])
    return x


def shifted(x, axis, s):
    n = lax.axis_size(axis)
    return lax.ppermute(x, axis, [(j, (j + s) % n) for j in range(n)])


def spread(stack, axis):
    n = lax.axis_size(axis)
    me = lax.axis_index(axis)
    mine = jnp.roll(stack, -me, axis=0)
    pieces = [mine[0]] + [shifted(mine[s], axis, s) for s in range(1, n)]
    ordered = jnp.stack([pieces[(-i) % n] for i in range(n)])
    return jnp.roll(ordered, me, axis=0)


def gather_all(x, axis):
    n = lax.axis_size(axis)
    me = lax.axis_index(axis)
    pieces = [x] + [shifted(x, axis, s) for s in range(1, n)]
    ordered = jnp.stack([pieces[(-i) % n] for i in range(n)])
    return jnp.roll(ordered, me, axis=0)


def ring_sum(x, axis):
    n = lax.axis_size(axis)
    parts = x.reshape(n, x.shape[0] // n, *x.shape[1:])
    own = lax.all_to_all(parts, axis, 0, 0, tiled=True).sum(axis=0)
    return collect(own, axis, 0)


def inner_gram(columns):
    return lax.dot_general(
        columns, columns, (((0,), (0,)), ((), ())), precision=lax.Precision.HIGHEST
    )


def mm(a, b):
    return jnp.dot(a, b, precision=lax.Precision.HIGHEST)


def _factor_kernel(a_ref, w_ref, r_ref, panel_rows):
    n = a_ref.shape[0]
    rows_i = lax.broadcasted_iota(jnp.int32, (n, n), 0)
    cols_i = lax.broadcasted_iota(jnp.int32, (n, n), 1)
    r_ref[:, :n] = a_ref[...]
    r_ref[:, n:] = jnp.where(rows_i == cols_i, 1.0, 0.0).astype(jnp.float32)
    sub = lax.broadcasted_iota(jnp.int32, (panel_rows, 1), 0)
    lane = lax.broadcasted_iota(jnp.int32, (panel_rows, 128), 1)
    lane_wide = lax.broadcasted_iota(jnp.int32, (1, 2 * n), 1)
    for p in range(n // panel_rows):
        r0 = panel_rows * p
        panel = r_ref[r0:r0 + panel_rows, :]
        for r in range(panel_rows):
            j = r0 + r
            part = panel[:, (j // 128) * 128:(j // 128 + 1) * 128]
            column = jnp.sum(jnp.where(lane == (j % 128), part, 0.0), axis=1, keepdims=True)
            inv = lax.rsqrt(column[r:r + 1, :])
            row = jnp.where(lane_wide < j, 0.0, panel[r:r + 1, :] * inv)
            mult = jnp.where(sub > r, column * inv, 0.0)
            panel = jnp.where(sub == r, row, panel - mult * row)
        r_ref[r0:r0 + panel_rows, :] = panel
        low = r0 + panel_rows
        if low < n:
            outer = lax.dot_general(
                panel[:, :n], panel, (((0,), (0,)), ((), ())),
                precision=lax.Precision.HIGHEST, preferred_element_type=jnp.float32,
            )
            r_ref[low:, :] = r_ref[low:, :] - outer[low:, :]
    w_ref[...] = r_ref[:, n:]


def inverse_factor(matrix):
    n = matrix.shape[0]
    sym = (matrix + matrix.T) * 0.5
    return pl.pallas_call(
        functools.partial(_factor_kernel, panel_rows=64),
        out_shape=jax.ShapeDtypeStruct((n, n), jnp.float32),
        scratch_shapes=[pltpu.VMEM((n, 2 * n), jnp.float32)],
    )(sym)


def cholesky_pass(columns, gram_matrix):
    return mm(columns, inverse_factor(gram_matrix).T)


def shards(inputs, out_grads, test_matrix, momentum):
    features = inputs[0]
    errors = out_grads[0]
    probes = test_matrix[0]
    replicas = lax.axis_size(DP)
    scale = 1.0 / (features.shape[1] * features.shape[0] * replicas)
    projected = jnp.dot(features, probes, preferred_element_type=jnp.float32).astype(jnp.bfloat16)
    token_gram = lax.dot_general(
        errors, errors, (((1,), (1,)), ((), ())), preferred_element_type=jnp.float32
    ).astype(jnp.bfloat16)
    mixed_rows = jnp.dot(token_gram, projected, preferred_element_type=jnp.float32).astype(
        jnp.bfloat16
    )
    sketch_term = (
        lax.dot_general(
            features, mixed_rows, (((0,), (0,)), ((), ())), preferred_element_type=jnp.float32
        )
        * scale
    )
    sketch = total_of(sketch_term, (("dp_0", "dp_1"), "dp_2")).astype(jnp.float32)
    basis = cholesky_pass(sketch, inner_gram(sketch)).astype(jnp.bfloat16)
    reduced = jnp.dot(features, basis, preferred_element_type=jnp.float32).astype(jnp.bfloat16)
    shaped = jnp.dot(token_gram, reduced, preferred_element_type=jnp.float32).astype(jnp.bfloat16)
    core_term = (
        lax.dot_general(
            reduced, shaped, (((0,), (0,)), ((), ())), preferred_element_type=jnp.float32
        )
        * scale
    )
    core_matrix = ring_sum(butterfly_sum(core_term, DP, (1, 16)), "dp_1")
    shifted = core_matrix + jnp.eye(core_matrix.shape[0], dtype=jnp.float32)
    inverse = inverse_factor(shifted)
    factor = mm(inverse.T, mm(inverse, core_matrix))
    blocks = spread(momentum, "blk")
    columns = blocks.reshape(-1, blocks.shape[-1])
    coeffs = lax.dot_general(
        basis, columns, (((0,), (0,)), ((), ())), preferred_element_type=jnp.float32
    )
    scaled = jnp.dot(factor, coeffs, precision=lax.Precision.HIGHEST).astype(jnp.bfloat16)
    fresh = (
        columns.astype(jnp.float32) - jnp.dot(basis, scaled, preferred_element_type=jnp.float32)
    ).astype(jnp.bfloat16)
    return spread(fresh.reshape(blocks.shape), "blk")


def solution(mesh):
    torus = Mesh(mesh.devices.reshape(2, 8, 2, mesh.shape["blk"]), ("dp_0", "dp_1", "dp_2", "blk"))
    in_specs = (P("blk", DP, None), P("blk", DP, None), P("blk", None, None), P(None, "blk", DP))
    out_specs = P(None, "blk", DP)
    return jax.shard_map(
        shards, mesh=torus, in_specs=in_specs, out_specs=out_specs, check_vma=False
    )
```

```python
import functools
import jax
import jax.numpy as jnp
from jax import lax
from jax.sharding import Mesh
from jax.sharding import PartitionSpec as P
from jax.experimental import pallas as pl
from jax.experimental.pallas import tpu as pltpu

DP = ("dp_0", "dp_1", "dp_2")


def filled_up(lines, devices):
    spare = -len(lines) % devices
    return jnp.pad(lines, [(0, spare)] + [(0, 0)] * (lines.ndim - 1))


def copy_for_each(x, axis):
    devices = lax.axis_size(axis)
    return lax.all_to_all(jnp.broadcast_to(x[None], (devices, *x.shape)), axis, 0, 0, tiled=True)


def in_order(blocks, dim):
    blocks = jnp.moveaxis(blocks, 0, dim)
    lengths = blocks.shape
    return blocks.reshape(*lengths[:dim], lengths[dim] * lengths[dim + 1], *lengths[dim + 2 :])


def whole_of(x, axes, dim):
    far, near = axes
    first = copy_for_each(x, far)
    blocks = jnp.swapaxes(copy_for_each(first, near), 0, 1)
    return in_order(blocks.reshape(-1, *x.shape), dim)


def in_blocks(x, dim, devices):
    lengths = x.shape
    blocks = x.reshape(*lengths[:dim], devices, lengths[dim] // devices, *lengths[dim + 1 :])
    return jnp.moveaxis(blocks, dim, 0)


def sum_at_owner(x, axis, dim):
    blocks = in_blocks(x, dim, lax.axis_size(axis))
    arrived = lax.all_to_all(blocks, axis, split_axis=0, concat_axis=0, tiled=True)
    return arrived.sum(axis=0)


def sum_by_axis(x, axes, dim):
    far, near = axes
    blocks = in_blocks(x, dim, lax.axis_size(far))
    nearer = sum_at_owner(blocks, near, dim + 1).astype(jnp.bfloat16)
    arrived = lax.all_to_all(nearer, far, split_axis=0, concat_axis=0, tiled=True)
    return arrived.astype(jnp.float32).sum(axis=0)


def total_of(x, axes):
    lines = x.reshape(-1, x.shape[-1])
    padded = filled_up(lines, lax.axis_size(axes[0]) * lax.axis_size(axes[1]))
    whole = whole_of(sum_by_axis(padded, axes, 0).astype(jnp.bfloat16), axes, 0)
    return lax.slice_in_dim(whole, 0, len(lines)).reshape(x.shape)


def collect(x, axis, dim):
    blocks = copy_for_each(x, axis)
    return in_order(blocks, dim)


def total_of_2(x, axes):
    lines = x.reshape(-1, x.shape[-1])
    own = sum_at_owner(filled_up(lines, lax.axis_size(axes)), axes, 0)
    whole = collect(own, axes, 0)
    return whole[: len(lines)].reshape(x.shape)


def butterfly_sum(x, axes, masks):
    size = 1
    for a in axes:
        size *= lax.axis_size(a)
    for m in masks:
        x = x + lax.ppermute(x, axes, [(i, i ^ m) for i in range(size)])
    return x


def shifted(x, axis, s):
    n = lax.axis_size(axis)
    return lax.ppermute(x, axis, [(j, (j + s) % n) for j in range(n)])


def spread(stack, axis):
    n = lax.axis_size(axis)
    me = lax.axis_index(axis)
    mine = jnp.roll(stack, -me, axis=0)
    pieces = [mine[0]] + [shifted(mine[s], axis, s) for s in range(1, n)]
    ordered = jnp.stack([pieces[(-i) % n] for i in range(n)])
    return jnp.roll(ordered, me, axis=0)


def gather_all(x, axis):
    n = lax.axis_size(axis)
    me = lax.axis_index(axis)
    pieces = [x] + [shifted(x, axis, s) for s in range(1, n)]
    ordered = jnp.stack([pieces[(-i) % n] for i in range(n)])
    return jnp.roll(ordered, me, axis=0)


def ring_sum(x, axis):
    n = lax.axis_size(axis)
    parts = x.reshape(n, x.shape[0] // n, *x.shape[1:])
    own = lax.all_to_all(parts, axis, 0, 0, tiled=True).sum(axis=0)
    return collect(own, axis, 0)


def inner_gram(columns):
    return lax.dot_general(
        columns, columns, (((0,), (0,)), ((), ())), precision=lax.Precision.HIGHEST
    )


def mm(a, b):
    return jnp.dot(a, b, precision=lax.Precision.HIGHEST)


def _factor_kernel(a_ref, w_ref, r_ref, panel_rows):
    n = a_ref.shape[0]
    rows_i = lax.broadcasted_iota(jnp.int32, (n, n), 0)
    cols_i = lax.broadcasted_iota(jnp.int32, (n, n), 1)
    r_ref[:, :n] = a_ref[...]
    r_ref[:, n:] = jnp.where(rows_i == cols_i, 1.0, 0.0).astype(jnp.float32)
    sub = lax.broadcasted_iota(jnp.int32, (panel_rows, 1), 0)
    lane_wide = lax.broadcasted_iota(jnp.int32, (1, 2 * n), 1)
    for p in range(n // panel_rows):
        r0 = panel_rows * p
        panel = r_ref[r0:r0 + panel_rows, :]
        for r in range(panel_rows):
            j = r0 + r
            part = panel[:, (j // 128) * 128:(j // 128 + 1) * 128]
            column = part[:, j % 128:j % 128 + 1]
            inv = lax.rsqrt(column[r:r + 1, :])
            row = jnp.where(lane_wide < j, 0.0, panel[r:r + 1, :] * inv)
            mult = jnp.where(sub > r, column * inv, 0.0)
            panel = jnp.where(sub == r, row, panel - mult * row)
        r_ref[r0:r0 + panel_rows, :] = panel
        low = r0 + panel_rows
        if low < n:
            outer = lax.dot_general(
                panel[:, :n], panel, (((0,), (0,)), ((), ())),
                precision=lax.Precision.HIGHEST, preferred_element_type=jnp.float32,
            )
            r_ref[low:, :] = r_ref[low:, :] - outer[low:, :]
    w_ref[...] = r_ref[:, n:]


def inverse_factor(matrix):
    n = matrix.shape[0]
    sym = (matrix + matrix.T) * 0.5
    return pl.pallas_call(
        functools.partial(_factor_kernel, panel_rows=64),
        out_shape=jax.ShapeDtypeStruct((n, n), jnp.float32),
        scratch_shapes=[pltpu.VMEM((n, 2 * n), jnp.float32)],
    )(sym)


def cholesky_pass(columns, gram_matrix):
    return mm(columns, inverse_factor(gram_matrix).T)


def shards(inputs, out_grads, test_matrix, momentum):
    features = inputs[0]
    errors = out_grads[0]
    probes = test_matrix[0]
    owners = momentum.shape[0]
    me = lax.axis_index("blk")
    mine = jnp.roll(momentum, -me, axis=0)
    pieces = [mine[0]] + [shifted(mine[s], "blk", s) for s in range(1, owners)]
    columns = jnp.concatenate(pieces, axis=0)
    replicas = lax.axis_size(DP)
    scale = 1.0 / (features.shape[1] * features.shape[0] * replicas)
    projected = jnp.dot(features, probes, preferred_element_type=jnp.float32).astype(jnp.bfloat16)
    token_gram = lax.dot_general(
        errors, errors, (((1,), (1,)), ((), ())), preferred_element_type=jnp.float32
    ).astype(jnp.bfloat16)
    mixed_rows = jnp.dot(token_gram, projected, preferred_element_type=jnp.float32).astype(
        jnp.bfloat16
    )
    sketch_term = (
        lax.dot_general(
            features, mixed_rows, (((0,), (0,)), ((), ())), preferred_element_type=jnp.float32
        )
        * scale
    )
    sketch = total_of(sketch_term, (("dp_0", "dp_1"), "dp_2")).astype(jnp.float32)
    basis = cholesky_pass(sketch, inner_gram(sketch)).astype(jnp.bfloat16)
    backward = basis.reshape(owners, -1, basis.shape[-1])[::-1]
    twice = jnp.concatenate([backward, backward], axis=0)
    basis_here = lax.dynamic_slice_in_dim(twice, owners - 1 - me, owners, axis=0).reshape(basis.shape)
    reduced = jnp.dot(features, basis, preferred_element_type=jnp.float32).astype(jnp.bfloat16)
    shaped = jnp.dot(token_gram, reduced, preferred_element_type=jnp.float32).astype(jnp.bfloat16)
    core_term = (
        lax.dot_general(
            reduced, shaped, (((0,), (0,)), ((), ())), preferred_element_type=jnp.float32
        )
        * scale
    )
    core_matrix = ring_sum(butterfly_sum(core_term, DP, (1, 16)), "dp_1")
    raised = core_matrix + jnp.eye(core_matrix.shape[0], dtype=jnp.float32)
    inverse = inverse_factor(raised)
    factor = mm(inverse.T, mm(inverse, core_matrix))
    coeffs = lax.dot_general(
        basis_here, columns, (((0,), (0,)), ((), ())), preferred_element_type=jnp.float32
    )
    scaled = jnp.dot(factor, coeffs, precision=lax.Precision.HIGHEST).astype(jnp.bfloat16)
    fresh = (
        columns.astype(jnp.float32) - jnp.dot(basis_here, scaled, preferred_element_type=jnp.float32)
    ).astype(jnp.bfloat16)
    parts = fresh.reshape(momentum.shape)
    back = [parts[0]] + [shifted(parts[s], "blk", owners - s) for s in range(1, owners)]
    return jnp.roll(jnp.stack(back), me, axis=0)


def solution(mesh):
    torus = Mesh(mesh.devices.reshape(2, 8, 2, mesh.shape["blk"]), ("dp_0", "dp_1", "dp_2", "blk"))
    in_specs = (P("blk", DP, None), P("blk", DP, None), P("blk", None, None), P(None, "blk", DP))
    out_specs = P(None, "blk", DP)
    return jax.shard_map(
        shards, mesh=torus, in_specs=in_specs, out_specs=out_specs, check_vma=False
    )
```

```python
import functools
import jax
import jax.numpy as jnp
from jax import lax
from jax.sharding import Mesh
from jax.sharding import PartitionSpec as P
from jax.experimental import pallas as pl
from jax.experimental.pallas import tpu as pltpu

DP = ("dp_0", "dp_1", "dp_2")


def filled_up(lines, devices):
    spare = -len(lines) % devices
    return jnp.pad(lines, [(0, spare)] + [(0, 0)] * (lines.ndim - 1))


def copy_for_each(x, axis):
    devices = lax.axis_size(axis)
    return lax.all_to_all(jnp.broadcast_to(x[None], (devices, *x.shape)), axis, 0, 0, tiled=True)


def in_order(blocks, dim):
    blocks = jnp.moveaxis(blocks, 0, dim)
    lengths = blocks.shape
    return blocks.reshape(*lengths[:dim], lengths[dim] * lengths[dim + 1], *lengths[dim + 2 :])


def whole_of(x, axes, dim):
    far, near = axes
    first = copy_for_each(x, far)
    blocks = jnp.swapaxes(copy_for_each(first, near), 0, 1)
    return in_order(blocks.reshape(-1, *x.shape), dim)


def in_blocks(x, dim, devices):
    lengths = x.shape
    blocks = x.reshape(*lengths[:dim], devices, lengths[dim] // devices, *lengths[dim + 1 :])
    return jnp.moveaxis(blocks, dim, 0)


def sum_at_owner(x, axis, dim):
    blocks = in_blocks(x, dim, lax.axis_size(axis))
    arrived = lax.all_to_all(blocks, axis, split_axis=0, concat_axis=0, tiled=True)
    return arrived.sum(axis=0)


def sum_by_axis(x, axes, dim):
    far, near = axes
    blocks = in_blocks(x, dim, lax.axis_size(far))
    nearer = sum_at_owner(blocks, near, dim + 1).astype(jnp.bfloat16)
    arrived = lax.all_to_all(nearer, far, split_axis=0, concat_axis=0, tiled=True)
    return arrived.astype(jnp.float32).sum(axis=0)


def total_of(x, axes):
    lines = x.reshape(-1, x.shape[-1])
    padded = filled_up(lines, lax.axis_size(axes[0]) * lax.axis_size(axes[1]))
    whole = whole_of(sum_by_axis(padded, axes, 0).astype(jnp.bfloat16), axes, 0)
    return lax.slice_in_dim(whole, 0, len(lines)).reshape(x.shape)


def collect(x, axis, dim):
    blocks = copy_for_each(x, axis)
    return in_order(blocks, dim)


def total_of_2(x, axes):
    lines = x.reshape(-1, x.shape[-1])
    own = sum_at_owner(filled_up(lines, lax.axis_size(axes)), axes, 0)
    whole = collect(own, axes, 0)
    return whole[: len(lines)].reshape(x.shape)


def butterfly_sum(x, axes, masks):
    size = 1
    for a in axes:
        size *= lax.axis_size(a)
    for m in masks:
        x = x + lax.ppermute(x, axes, [(i, i ^ m) for i in range(size)])
    return x


def shifted(x, axis, s):
    n = lax.axis_size(axis)
    return lax.ppermute(x, axis, [(j, (j + s) % n) for j in range(n)])


def spread(stack, axis):
    n = lax.axis_size(axis)
    me = lax.axis_index(axis)
    mine = jnp.roll(stack, -me, axis=0)
    pieces = [mine[0]] + [shifted(mine[s], axis, s) for s in range(1, n)]
    ordered = jnp.stack([pieces[(-i) % n] for i in range(n)])
    return jnp.roll(ordered, me, axis=0)


def gather_all(x, axis):
    n = lax.axis_size(axis)
    me = lax.axis_index(axis)
    pieces = [x] + [shifted(x, axis, s) for s in range(1, n)]
    ordered = jnp.stack([pieces[(-i) % n] for i in range(n)])
    return jnp.roll(ordered, me, axis=0)


def ring_sum(x, axis):
    n = lax.axis_size(axis)
    parts = x.reshape(n, x.shape[0] // n, *x.shape[1:])
    own = lax.all_to_all(parts, axis, 0, 0, tiled=True).sum(axis=0)
    return collect(own, axis, 0)


def inner_gram(columns):
    return lax.dot_general(
        columns, columns, (((0,), (0,)), ((), ())), precision=lax.Precision.HIGHEST
    )


def mm(a, b):
    return jnp.dot(a, b, precision=lax.Precision.HIGHEST)


def _factor_kernel(a_ref, w_ref, r_ref, panel_rows):
    n = a_ref.shape[0]
    rows_i = lax.broadcasted_iota(jnp.int32, (n, n), 0)
    cols_i = lax.broadcasted_iota(jnp.int32, (n, n), 1)
    r_ref[:, :n] = a_ref[...]
    r_ref[:, n:] = jnp.where(rows_i == cols_i, 1.0, 0.0).astype(jnp.float32)
    sub = lax.broadcasted_iota(jnp.int32, (panel_rows, 1), 0)
    lane_wide = lax.broadcasted_iota(jnp.int32, (1, 2 * n), 1)
    for p in range(n // panel_rows):
        r0 = panel_rows * p
        panel = r_ref[r0:r0 + panel_rows, :]
        for r in range(panel_rows):
            j = r0 + r
            part = panel[:, (j // 128) * 128:(j // 128 + 1) * 128]
            column = part[:, j % 128:j % 128 + 1]
            inv = lax.rsqrt(column[r:r + 1, :])
            row = jnp.where(lane_wide < j, 0.0, panel[r:r + 1, :] * inv)
            mult = jnp.where(sub > r, column * inv, 0.0)
            panel = jnp.where(sub == r, row, panel - mult * row)
        r_ref[r0:r0 + panel_rows, :] = panel
        low = r0 + panel_rows
        if low < n:
            outer = lax.dot_general(
                panel[:, :n], panel, (((0,), (0,)), ((), ())),
                precision=lax.Precision.HIGHEST, preferred_element_type=jnp.float32,
            )
            r_ref[low:, :] = r_ref[low:, :] - outer[low:, :]
    w_ref[...] = r_ref[:, n:]


def inverse_factor(matrix):
    n = matrix.shape[0]
    sym = (matrix + matrix.T) * 0.5
    return pl.pallas_call(
        functools.partial(_factor_kernel, panel_rows=64),
        out_shape=jax.ShapeDtypeStruct((n, n), jnp.float32),
        scratch_shapes=[pltpu.VMEM((n, 2 * n), jnp.float32)],
    )(sym)


def cholesky_pass(columns, gram_matrix):
    return mm(columns, inverse_factor(gram_matrix).T)


def shards(inputs, out_grads, test_matrix, momentum):
    features = inputs[0]
    errors = out_grads[0]
    probes = test_matrix[0]
    replicas = lax.axis_size(DP)
    scale = 1.0 / (features.shape[1] * features.shape[0] * replicas)
    projected = jnp.dot(features, probes, preferred_element_type=jnp.float32).astype(jnp.bfloat16)
    token_gram = lax.dot_general(
        errors, errors, (((1,), (1,)), ((), ())), preferred_element_type=jnp.float32
    ).astype(jnp.bfloat16)
    mixed_rows = jnp.dot(token_gram, projected, preferred_element_type=jnp.float32).astype(
        jnp.bfloat16
    )
    sketch_term = (
        lax.dot_general(
            features, mixed_rows, (((0,), (0,)), ((), ())), preferred_element_type=jnp.float32
        )
        * scale
    )
    sketch = total_of(sketch_term, (("dp_0", "dp_1"), "dp_2")).astype(jnp.float32)
    basis = cholesky_pass(sketch, inner_gram(sketch)).astype(jnp.bfloat16)
    reduced = jnp.dot(features, basis, preferred_element_type=jnp.float32).astype(jnp.bfloat16)
    shaped = jnp.dot(token_gram, reduced, preferred_element_type=jnp.float32).astype(jnp.bfloat16)
    core_term = (
        lax.dot_general(
            reduced, shaped, (((0,), (0,)), ((), ())), preferred_element_type=jnp.float32
        )
        * scale
    )
    core_matrix = ring_sum(butterfly_sum(core_term, DP, (1, 16)), "dp_1")
    shifted = core_matrix + jnp.eye(core_matrix.shape[0], dtype=jnp.float32)
    inverse = inverse_factor(shifted)
    factor = mm(inverse.T, mm(inverse, core_matrix))
    blocks = spread(momentum, "blk")
    columns = blocks.reshape(-1, blocks.shape[-1])
    coeffs = lax.dot_general(
        basis, columns, (((0,), (0,)), ((), ())), preferred_element_type=jnp.float32
    )
    scaled = jnp.dot(factor, coeffs, precision=lax.Precision.HIGHEST).astype(jnp.bfloat16)
    fresh = (
        columns.astype(jnp.float32) - jnp.dot(basis, scaled, preferred_element_type=jnp.float32)
    ).astype(jnp.bfloat16)
    return spread(fresh.reshape(blocks.shape), "blk")


def solution(mesh):
    torus = Mesh(mesh.devices.reshape(2, 8, 2, mesh.shape["blk"]), ("dp_0", "dp_1", "dp_2", "blk"))
    in_specs = (P("blk", DP, None), P("blk", DP, None), P("blk", None, None), P(None, "blk", DP))
    out_specs = P(None, "blk", DP)
    return jax.shard_map(
        shards, mesh=torus, in_specs=in_specs, out_specs=out_specs, check_vma=False
    )
```

```python
import functools
import jax
import jax.numpy as jnp
from jax import lax
from jax.sharding import Mesh
from jax.sharding import PartitionSpec as P
from jax.experimental import pallas as pl
from jax.experimental.pallas import tpu as pltpu

DP = ("dp_0", "dp_1", "dp_2")


def filled_up(lines, devices):
    spare = -len(lines) % devices
    return jnp.pad(lines, [(0, spare)] + [(0, 0)] * (lines.ndim - 1))


def copy_for_each(x, axis):
    devices = lax.axis_size(axis)
    return lax.all_to_all(jnp.broadcast_to(x[None], (devices, *x.shape)), axis, 0, 0, tiled=True)


def in_order(blocks, dim):
    blocks = jnp.moveaxis(blocks, 0, dim)
    lengths = blocks.shape
    return blocks.reshape(*lengths[:dim], lengths[dim] * lengths[dim + 1], *lengths[dim + 2 :])


def whole_of(x, axes, dim):
    far, near = axes
    first = copy_for_each(x, far)
    blocks = jnp.swapaxes(copy_for_each(first, near), 0, 1)
    return in_order(blocks.reshape(-1, *x.shape), dim)


def in_blocks(x, dim, devices):
    lengths = x.shape
    blocks = x.reshape(*lengths[:dim], devices, lengths[dim] // devices, *lengths[dim + 1 :])
    return jnp.moveaxis(blocks, dim, 0)


def sum_at_owner(x, axis, dim):
    blocks = in_blocks(x, dim, lax.axis_size(axis))
    arrived = lax.all_to_all(blocks, axis, split_axis=0, concat_axis=0, tiled=True)
    return arrived.sum(axis=0)


def sum_by_axis(x, axes, dim):
    far, near = axes
    blocks = in_blocks(x, dim, lax.axis_size(far))
    nearer = sum_at_owner(blocks, near, dim + 1).astype(jnp.bfloat16)
    arrived = lax.all_to_all(nearer, far, split_axis=0, concat_axis=0, tiled=True)
    return arrived.astype(jnp.float32).sum(axis=0)


def total_of(x, axes):
    lines = x.reshape(-1, x.shape[-1])
    padded = filled_up(lines, lax.axis_size(axes[0]) * lax.axis_size(axes[1]))
    whole = whole_of(sum_by_axis(padded, axes, 0).astype(jnp.bfloat16), axes, 0)
    return lax.slice_in_dim(whole, 0, len(lines)).reshape(x.shape)


def chip_first_sum(x, far, near):
    me = lax.axis_index(near)
    halves = x.reshape(2, -1, x.shape[-1])
    kept = lax.dynamic_index_in_dim(halves, me, 0, keepdims=False)
    given = lax.dynamic_index_in_dim(halves, 1 - me, 0, keepdims=False)
    nearer = kept + lax.ppermute(given, near, [(0, 1), (1, 0)])
    blocks = in_blocks(nearer, 0, lax.axis_size(far)).astype(jnp.bfloat16)
    arrived = lax.all_to_all(blocks, far, split_axis=0, concat_axis=0, tiled=True)
    own = arrived.astype(jnp.float32).sum(axis=0).astype(jnp.bfloat16)
    first = copy_for_each(own, far)
    return in_order(copy_for_each(first, near).reshape(-1, *own.shape), 0)


def collect(x, axis, dim):
    blocks = copy_for_each(x, axis)
    return in_order(blocks, dim)


def total_of_2(x, axes):
    lines = x.reshape(-1, x.shape[-1])
    own = sum_at_owner(filled_up(lines, lax.axis_size(axes)), axes, 0)
    whole = collect(own, axes, 0)
    return whole[: len(lines)].reshape(x.shape)


def butterfly_sum(x, axes, masks):
    size = 1
    for a in axes:
        size *= lax.axis_size(a)
    for m in masks:
        x = x + lax.ppermute(x, axes, [(i, i ^ m) for i in range(size)])
    return x


def shifted(x, axis, s):
    n = lax.axis_size(axis)
    return lax.ppermute(x, axis, [(j, (j + s) % n) for j in range(n)])


def spread(stack, axis):
    n = lax.axis_size(axis)
    me = lax.axis_index(axis)
    mine = jnp.roll(stack, -me, axis=0)
    pieces = [mine[0]] + [shifted(mine[s], axis, s) for s in range(1, n)]
    ordered = jnp.stack([pieces[(-i) % n] for i in range(n)])
    return jnp.roll(ordered, me, axis=0)


def gather_all(x, axis):
    n = lax.axis_size(axis)
    me = lax.axis_index(axis)
    pieces = [x] + [shifted(x, axis, s) for s in range(1, n)]
    ordered = jnp.stack([pieces[(-i) % n] for i in range(n)])
    return jnp.roll(ordered, me, axis=0)


def ring_sum(x, axis):
    n = lax.axis_size(axis)
    parts = x.reshape(n, x.shape[0] // n, *x.shape[1:])
    own = lax.all_to_all(parts, axis, 0, 0, tiled=True).sum(axis=0)
    return collect(own, axis, 0)


def inner_gram(columns):
    return lax.dot_general(
        columns, columns, (((0,), (0,)), ((), ())), precision=lax.Precision.HIGHEST
    )


def mm(a, b):
    return jnp.dot(a, b, precision=lax.Precision.HIGHEST)


def _factor_kernel(a_ref, w_ref, r_ref, panel_rows):
    n = a_ref.shape[0]
    rows_i = lax.broadcasted_iota(jnp.int32, (n, n), 0)
    cols_i = lax.broadcasted_iota(jnp.int32, (n, n), 1)
    r_ref[:, :n] = a_ref[...]
    r_ref[:, n:] = jnp.where(rows_i == cols_i, 1.0, 0.0).astype(jnp.float32)
    sub = lax.broadcasted_iota(jnp.int32, (panel_rows, 1), 0)
    lane_wide = lax.broadcasted_iota(jnp.int32, (1, 2 * n), 1)
    for p in range(n // panel_rows):
        r0 = panel_rows * p
        panel = r_ref[r0:r0 + panel_rows, :]
        for r in range(panel_rows):
            j = r0 + r
            part = panel[:, (j // 128) * 128:(j // 128 + 1) * 128]
            column = part[:, j % 128:j % 128 + 1]
            inv = lax.rsqrt(column[r:r + 1, :])
            row = jnp.where(lane_wide < j, 0.0, panel[r:r + 1, :] * inv)
            mult = jnp.where(sub > r, column * inv, 0.0)
            panel = jnp.where(sub == r, row, panel - mult * row)
        r_ref[r0:r0 + panel_rows, :] = panel
        low = r0 + panel_rows
        if low < n:
            outer = lax.dot_general(
                panel[:, :n], panel, (((0,), (0,)), ((), ())),
                precision=lax.Precision.HIGHEST, preferred_element_type=jnp.float32,
            )
            r_ref[low:, :] = r_ref[low:, :] - outer[low:, :]
    w_ref[...] = r_ref[:, n:]


def inverse_factor(matrix):
    n = matrix.shape[0]
    sym = (matrix + matrix.T) * 0.5
    return pl.pallas_call(
        functools.partial(_factor_kernel, panel_rows=64),
        out_shape=jax.ShapeDtypeStruct((n, n), jnp.float32),
        scratch_shapes=[pltpu.VMEM((n, 2 * n), jnp.float32)],
    )(sym)


def cholesky_pass(columns, gram_matrix):
    return mm(columns, inverse_factor(gram_matrix).T)


def shards(inputs, out_grads, test_matrix, momentum):
    features = inputs[0]
    errors = out_grads[0]
    probes = test_matrix[0]
    replicas = lax.axis_size(DP)
    scale = 1.0 / (features.shape[1] * features.shape[0] * replicas)
    projected = jnp.dot(features, probes, preferred_element_type=jnp.float32).astype(jnp.bfloat16)
    token_gram = lax.dot_general(
        errors, errors, (((1,), (1,)), ((), ())), preferred_element_type=jnp.float32
    ).astype(jnp.bfloat16)
    mixed_rows = jnp.dot(token_gram, projected, preferred_element_type=jnp.float32).astype(
        jnp.bfloat16
    )
    sketch_term = (
        lax.dot_general(
            features, mixed_rows, (((0,), (0,)), ((), ())), preferred_element_type=jnp.float32
        )
        * scale
    )
    sketch = chip_first_sum(sketch_term, ("dp_0", "dp_1"), "dp_2").astype(jnp.float32)
    basis = cholesky_pass(sketch, inner_gram(sketch)).astype(jnp.bfloat16)
    reduced = jnp.dot(features, basis, preferred_element_type=jnp.float32).astype(jnp.bfloat16)
    shaped = jnp.dot(token_gram, reduced, preferred_element_type=jnp.float32).astype(jnp.bfloat16)
    core_term = (
        lax.dot_general(
            reduced, shaped, (((0,), (0,)), ((), ())), preferred_element_type=jnp.float32
        )
        * scale
    )
    core_matrix = ring_sum(butterfly_sum(core_term, DP, (1, 16)), "dp_1")
    shifted = core_matrix + jnp.eye(core_matrix.shape[0], dtype=jnp.float32)
    inverse = inverse_factor(shifted)
    factor = mm(inverse.T, mm(inverse, core_matrix))
    blocks = spread(momentum, "blk")
    columns = blocks.reshape(-1, blocks.shape[-1])
    coeffs = lax.dot_general(
        basis, columns, (((0,), (0,)), ((), ())), preferred_element_type=jnp.float32
    )
    scaled = jnp.dot(factor, coeffs, precision=lax.Precision.HIGHEST).astype(jnp.bfloat16)
    fresh = (
        columns.astype(jnp.float32) - jnp.dot(basis, scaled, preferred_element_type=jnp.float32)
    ).astype(jnp.bfloat16)
    return spread(fresh.reshape(blocks.shape), "blk")


def solution(mesh):
    torus = Mesh(mesh.devices.reshape(2, 8, 2, mesh.shape["blk"]), ("dp_0", "dp_1", "dp_2", "blk"))
    in_specs = (P("blk", DP, None), P("blk", DP, None), P("blk", None, None), P(None, "blk", DP))
    out_specs = P(None, "blk", DP)
    return jax.shard_map(
        shards, mesh=torus, in_specs=in_specs, out_specs=out_specs, check_vma=False
    )
```

```python
import functools
import jax
import jax.numpy as jnp
from jax import lax
from jax.sharding import Mesh
from jax.sharding import PartitionSpec as P
from jax.experimental import pallas as pl
from jax.experimental.pallas import tpu as pltpu

DP = ("dp_0", "dp_1", "dp_2")


def filled_up(lines, devices):
    spare = -len(lines) % devices
    return jnp.pad(lines, [(0, spare)] + [(0, 0)] * (lines.ndim - 1))


def copy_for_each(x, axis):
    devices = lax.axis_size(axis)
    return lax.all_to_all(jnp.broadcast_to(x[None], (devices, *x.shape)), axis, 0, 0, tiled=True)


def in_order(blocks, dim):
    blocks = jnp.moveaxis(blocks, 0, dim)
    lengths = blocks.shape
    return blocks.reshape(*lengths[:dim], lengths[dim] * lengths[dim + 1], *lengths[dim + 2 :])


def whole_of(x, axes, dim):
    far, near = axes
    first = copy_for_each(x, far)
    blocks = jnp.swapaxes(copy_for_each(first, near), 0, 1)
    return in_order(blocks.reshape(-1, *x.shape), dim)


def in_blocks(x, dim, devices):
    lengths = x.shape
    blocks = x.reshape(*lengths[:dim], devices, lengths[dim] // devices, *lengths[dim + 1 :])
    return jnp.moveaxis(blocks, dim, 0)


def sum_at_owner(x, axis, dim):
    blocks = in_blocks(x, dim, lax.axis_size(axis))
    arrived = lax.all_to_all(blocks, axis, split_axis=0, concat_axis=0, tiled=True)
    return arrived.sum(axis=0)


def sum_by_axis(x, axes, dim):
    far, near = axes
    blocks = in_blocks(x, dim, lax.axis_size(far))
    nearer = sum_at_owner(blocks, near, dim + 1).astype(jnp.bfloat16)
    arrived = lax.all_to_all(nearer, far, split_axis=0, concat_axis=0, tiled=True)
    return arrived.astype(jnp.float32).sum(axis=0)


def total_of(x, axes):
    lines = x.reshape(-1, x.shape[-1])
    padded = filled_up(lines, lax.axis_size(axes[0]) * lax.axis_size(axes[1]))
    whole = whole_of(sum_by_axis(padded, axes, 0).astype(jnp.bfloat16), axes, 0)
    return lax.slice_in_dim(whole, 0, len(lines)).reshape(x.shape)


def chip_first_sum(x, far, near):
    halves = x.reshape(lax.axis_size(near), -1, x.shape[-1])
    nearer = lax.all_to_all(halves, near, split_axis=0, concat_axis=0, tiled=True).sum(axis=0)
    blocks = in_blocks(nearer, 0, lax.axis_size(far)).astype(jnp.bfloat16)
    arrived = lax.all_to_all(blocks, far, split_axis=0, concat_axis=0, tiled=True)
    own = arrived.astype(jnp.float32).sum(axis=0).astype(jnp.bfloat16)
    first = copy_for_each(own, far)
    return in_order(copy_for_each(first, near).reshape(-1, *own.shape), 0)


def collect(x, axis, dim):
    blocks = copy_for_each(x, axis)
    return in_order(blocks, dim)


def total_of_2(x, axes):
    lines = x.reshape(-1, x.shape[-1])
    own = sum_at_owner(filled_up(lines, lax.axis_size(axes)), axes, 0)
    whole = collect(own, axes, 0)
    return whole[: len(lines)].reshape(x.shape)


def butterfly_sum(x, axes, masks):
    size = 1
    for a in axes:
        size *= lax.axis_size(a)
    for m in masks:
        x = x + lax.ppermute(x, axes, [(i, i ^ m) for i in range(size)])
    return x


def shifted(x, axis, s):
    n = lax.axis_size(axis)
    return lax.ppermute(x, axis, [(j, (j + s) % n) for j in range(n)])


def spread(stack, axis):
    n = lax.axis_size(axis)
    me = lax.axis_index(axis)
    mine = jnp.roll(stack, -me, axis=0)
    pieces = [mine[0]] + [shifted(mine[s], axis, s) for s in range(1, n)]
    ordered = jnp.stack([pieces[(-i) % n] for i in range(n)])
    return jnp.roll(ordered, me, axis=0)


def gather_all(x, axis):
    n = lax.axis_size(axis)
    me = lax.axis_index(axis)
    pieces = [x] + [shifted(x, axis, s) for s in range(1, n)]
    ordered = jnp.stack([pieces[(-i) % n] for i in range(n)])
    return jnp.roll(ordered, me, axis=0)


def ring_sum(x, axis):
    n = lax.axis_size(axis)
    parts = x.reshape(n, x.shape[0] // n, *x.shape[1:])
    own = lax.all_to_all(parts, axis, 0, 0, tiled=True).sum(axis=0)
    return collect(own, axis, 0)


def inner_gram(columns):
    return lax.dot_general(
        columns, columns, (((0,), (0,)), ((), ())), precision=lax.Precision.HIGHEST
    )


def mm(a, b):
    return jnp.dot(a, b, precision=lax.Precision.HIGHEST)


def _factor_kernel(a_ref, w_ref, r_ref, panel_rows):
    n = a_ref.shape[0]
    rows_i = lax.broadcasted_iota(jnp.int32, (n, n), 0)
    cols_i = lax.broadcasted_iota(jnp.int32, (n, n), 1)
    r_ref[:, :n] = a_ref[...]
    r_ref[:, n:] = jnp.where(rows_i == cols_i, 1.0, 0.0).astype(jnp.float32)
    sub = lax.broadcasted_iota(jnp.int32, (panel_rows, 1), 0)
    lane_wide = lax.broadcasted_iota(jnp.int32, (1, 2 * n), 1)
    for p in range(n // panel_rows):
        r0 = panel_rows * p
        panel = r_ref[r0:r0 + panel_rows, :]
        for r in range(panel_rows):
            j = r0 + r
            part = panel[:, (j // 128) * 128:(j // 128 + 1) * 128]
            column = part[:, j % 128:j % 128 + 1]
            inv = lax.rsqrt(column[r:r + 1, :])
            row = jnp.where(lane_wide < j, 0.0, panel[r:r + 1, :] * inv)
            mult = jnp.where(sub > r, column * inv, 0.0)
            panel = jnp.where(sub == r, row, panel - mult * row)
        r_ref[r0:r0 + panel_rows, :] = panel
        low = r0 + panel_rows
        if low < n:
            outer = lax.dot_general(
                panel[:, :n], panel, (((0,), (0,)), ((), ())),
                precision=lax.Precision.HIGHEST, preferred_element_type=jnp.float32,
            )
            r_ref[low:, :] = r_ref[low:, :] - outer[low:, :]
    w_ref[...] = r_ref[:, n:]


def inverse_factor(matrix):
    n = matrix.shape[0]
    sym = (matrix + matrix.T) * 0.5
    return pl.pallas_call(
        functools.partial(_factor_kernel, panel_rows=64),
        out_shape=jax.ShapeDtypeStruct((n, n), jnp.float32),
        scratch_shapes=[pltpu.VMEM((n, 2 * n), jnp.float32)],
    )(sym)


def cholesky_pass(columns, gram_matrix):
    return mm(columns, inverse_factor(gram_matrix).T)


def shards(inputs, out_grads, test_matrix, momentum):
    features = inputs[0]
    errors = out_grads[0]
    probes = test_matrix[0]
    replicas = lax.axis_size(DP)
    scale = 1.0 / (features.shape[1] * features.shape[0] * replicas)
    projected = jnp.dot(features, probes, preferred_element_type=jnp.float32).astype(jnp.bfloat16)
    token_gram = lax.dot_general(
        errors, errors, (((1,), (1,)), ((), ())), preferred_element_type=jnp.float32
    ).astype(jnp.bfloat16)
    mixed_rows = jnp.dot(token_gram, projected, preferred_element_type=jnp.float32).astype(
        jnp.bfloat16
    )
    sketch_term = (
        lax.dot_general(
            features, mixed_rows, (((0,), (0,)), ((), ())), preferred_element_type=jnp.float32
        )
        * scale
    )
    sketch = chip_first_sum(sketch_term, ("dp_0", "dp_1"), "dp_2").astype(jnp.float32)
    basis = cholesky_pass(sketch, inner_gram(sketch)).astype(jnp.bfloat16)
    reduced = jnp.dot(features, basis, preferred_element_type=jnp.float32).astype(jnp.bfloat16)
    shaped = jnp.dot(token_gram, reduced, preferred_element_type=jnp.float32).astype(jnp.bfloat16)
    core_term = (
        lax.dot_general(
            reduced, shaped, (((0,), (0,)), ((), ())), preferred_element_type=jnp.float32
        )
        * scale
    )
    core_matrix = ring_sum(butterfly_sum(core_term, DP, (1, 16)), "dp_1")
    shifted = core_matrix + jnp.eye(core_matrix.shape[0], dtype=jnp.float32)
    inverse = inverse_factor(shifted)
    factor = mm(inverse.T, mm(inverse, core_matrix))
    blocks = spread(momentum, "blk")
    columns = blocks.reshape(-1, blocks.shape[-1])
    coeffs = lax.dot_general(
        basis, columns, (((0,), (0,)), ((), ())), preferred_element_type=jnp.float32
    )
    scaled = jnp.dot(factor, coeffs, precision=lax.Precision.HIGHEST).astype(jnp.bfloat16)
    fresh = (
        columns.astype(jnp.float32) - jnp.dot(basis, scaled, preferred_element_type=jnp.float32)
    ).astype(jnp.bfloat16)
    return spread(fresh.reshape(blocks.shape), "blk")


def solution(mesh):
    torus = Mesh(mesh.devices.reshape(2, 8, 2, mesh.shape["blk"]), ("dp_0", "dp_1", "dp_2", "blk"))
    in_specs = (P("blk", DP, None), P("blk", DP, None), P("blk", None, None), P(None, "blk", DP))
    out_specs = P(None, "blk", DP)
    return jax.shard_map(
        shards, mesh=torus, in_specs=in_specs, out_specs=out_specs, check_vma=False
    )
```

```python
import functools
import jax
import jax.numpy as jnp
from jax import lax
from jax.sharding import Mesh
from jax.sharding import PartitionSpec as P
from jax.experimental import pallas as pl
from jax.experimental.pallas import tpu as pltpu

DP = ("dp_0", "dp_1", "dp_2")


def filled_up(lines, devices):
    spare = -len(lines) % devices
    return jnp.pad(lines, [(0, spare)] + [(0, 0)] * (lines.ndim - 1))


def copy_for_each(x, axis):
    devices = lax.axis_size(axis)
    return lax.all_to_all(jnp.broadcast_to(x[None], (devices, *x.shape)), axis, 0, 0, tiled=True)


def in_order(blocks, dim):
    blocks = jnp.moveaxis(blocks, 0, dim)
    lengths = blocks.shape
    return blocks.reshape(*lengths[:dim], lengths[dim] * lengths[dim + 1], *lengths[dim + 2 :])


def whole_of(x, axes, dim):
    far, near = axes
    first = copy_for_each(x, far)
    blocks = jnp.swapaxes(copy_for_each(first, near), 0, 1)
    return in_order(blocks.reshape(-1, *x.shape), dim)


def in_blocks(x, dim, devices):
    lengths = x.shape
    blocks = x.reshape(*lengths[:dim], devices, lengths[dim] // devices, *lengths[dim + 1 :])
    return jnp.moveaxis(blocks, dim, 0)


def sum_at_owner(x, axis, dim):
    blocks = in_blocks(x, dim, lax.axis_size(axis))
    arrived = lax.all_to_all(blocks, axis, split_axis=0, concat_axis=0, tiled=True)
    return arrived.sum(axis=0)


def sum_by_axis(x, axes, dim):
    far, near = axes
    blocks = in_blocks(x, dim, lax.axis_size(far))
    nearer = sum_at_owner(blocks, near, dim + 1).astype(jnp.bfloat16)
    arrived = lax.all_to_all(nearer, far, split_axis=0, concat_axis=0, tiled=True)
    return arrived.astype(jnp.float32).sum(axis=0)


def total_of(x, axes):
    lines = x.reshape(-1, x.shape[-1])
    padded = filled_up(lines, lax.axis_size(axes[0]) * lax.axis_size(axes[1]))
    whole = whole_of(sum_by_axis(padded, axes, 0).astype(jnp.bfloat16), axes, 0)
    return lax.slice_in_dim(whole, 0, len(lines)).reshape(x.shape)


def chip_first_sum(x, far, near):
    halves = x.reshape(lax.axis_size(near), -1, x.shape[-1])
    nearer = lax.all_to_all(halves, near, split_axis=0, concat_axis=0, tiled=True).sum(axis=0)
    outer_axis, inner_axis = far
    blocks = nearer.reshape(lax.axis_size(outer_axis), -1, *nearer.shape[1:])
    crossed = lax.all_to_all(blocks.astype(jnp.bfloat16), outer_axis, 0, 0, tiled=True)
    partial = crossed.astype(jnp.float32).sum(axis=0)
    parts = partial.reshape(lax.axis_size(inner_axis), -1, *partial.shape[1:])
    arrived = lax.all_to_all(parts.astype(jnp.bfloat16), inner_axis, 0, 0, tiled=True)
    own = arrived.astype(jnp.float32).sum(axis=0).astype(jnp.bfloat16)
    first = copy_for_each(own, far)
    return in_order(copy_for_each(first, near).reshape(-1, *own.shape), 0)


def collect(x, axis, dim):
    blocks = copy_for_each(x, axis)
    return in_order(blocks, dim)


def total_of_2(x, axes):
    lines = x.reshape(-1, x.shape[-1])
    own = sum_at_owner(filled_up(lines, lax.axis_size(axes)), axes, 0)
    whole = collect(own, axes, 0)
    return whole[: len(lines)].reshape(x.shape)


def butterfly_sum(x, axes, masks):
    size = 1
    for a in axes:
        size *= lax.axis_size(a)
    for m in masks:
        x = x + lax.ppermute(x, axes, [(i, i ^ m) for i in range(size)])
    return x


def shifted(x, axis, s):
    n = lax.axis_size(axis)
    return lax.ppermute(x, axis, [(j, (j + s) % n) for j in range(n)])


def spread(stack, axis):
    n = lax.axis_size(axis)
    me = lax.axis_index(axis)
    mine = jnp.roll(stack, -me, axis=0)
    pieces = [mine[0]] + [shifted(mine[s], axis, s) for s in range(1, n)]
    ordered = jnp.stack([pieces[(-i) % n] for i in range(n)])
    return jnp.roll(ordered, me, axis=0)


def gather_all(x, axis):
    n = lax.axis_size(axis)
    me = lax.axis_index(axis)
    pieces = [x] + [shifted(x, axis, s) for s in range(1, n)]
    ordered = jnp.stack([pieces[(-i) % n] for i in range(n)])
    return jnp.roll(ordered, me, axis=0)


def ring_sum(x, axis):
    n = lax.axis_size(axis)
    parts = x.reshape(n, x.shape[0] // n, *x.shape[1:])
    own = lax.all_to_all(parts, axis, 0, 0, tiled=True).sum(axis=0)
    return collect(own, axis, 0)


def inner_gram(columns):
    return lax.dot_general(
        columns, columns, (((0,), (0,)), ((), ())), precision=lax.Precision.HIGHEST
    )


def mm(a, b):
    return jnp.dot(a, b, precision=lax.Precision.HIGHEST)


def _factor_kernel(a_ref, w_ref, r_ref, panel_rows):
    n = a_ref.shape[0]
    rows_i = lax.broadcasted_iota(jnp.int32, (n, n), 0)
    cols_i = lax.broadcasted_iota(jnp.int32, (n, n), 1)
    r_ref[:, :n] = a_ref[...]
    r_ref[:, n:] = jnp.where(rows_i == cols_i, 1.0, 0.0).astype(jnp.float32)
    sub = lax.broadcasted_iota(jnp.int32, (panel_rows, 1), 0)
    lane_wide = lax.broadcasted_iota(jnp.int32, (1, 2 * n), 1)
    for p in range(n // panel_rows):
        r0 = panel_rows * p
        panel = r_ref[r0:r0 + panel_rows, :]
        for r in range(panel_rows):
            j = r0 + r
            part = panel[:, (j // 128) * 128:(j // 128 + 1) * 128]
            column = part[:, j % 128:j % 128 + 1]
            inv = lax.rsqrt(column[r:r + 1, :])
            row = jnp.where(lane_wide < j, 0.0, panel[r:r + 1, :] * inv)
            mult = jnp.where(sub > r, column * inv, 0.0)
            panel = jnp.where(sub == r, row, panel - mult * row)
        r_ref[r0:r0 + panel_rows, :] = panel
        low = r0 + panel_rows
        if low < n:
            outer = lax.dot_general(
                panel[:, :n], panel, (((0,), (0,)), ((), ())),
                precision=lax.Precision.HIGHEST, preferred_element_type=jnp.float32,
            )
            r_ref[low:, :] = r_ref[low:, :] - outer[low:, :]
    w_ref[...] = r_ref[:, n:]


def inverse_factor(matrix):
    n = matrix.shape[0]
    sym = (matrix + matrix.T) * 0.5
    return pl.pallas_call(
        functools.partial(_factor_kernel, panel_rows=64),
        out_shape=jax.ShapeDtypeStruct((n, n), jnp.float32),
        scratch_shapes=[pltpu.VMEM((n, 2 * n), jnp.float32)],
    )(sym)


def cholesky_pass(columns, gram_matrix):
    return mm(columns, inverse_factor(gram_matrix).T)


def shards(inputs, out_grads, test_matrix, momentum):
    features = inputs[0]
    errors = out_grads[0]
    probes = test_matrix[0]
    replicas = lax.axis_size(DP)
    scale = 1.0 / (features.shape[1] * features.shape[0] * replicas)
    projected = jnp.dot(features, probes, preferred_element_type=jnp.float32).astype(jnp.bfloat16)
    token_gram = lax.dot_general(
        errors, errors, (((1,), (1,)), ((), ())), preferred_element_type=jnp.float32
    ).astype(jnp.bfloat16)
    mixed_rows = jnp.dot(token_gram, projected, preferred_element_type=jnp.float32).astype(
        jnp.bfloat16
    )
    sketch_term = (
        lax.dot_general(
            features, mixed_rows, (((0,), (0,)), ((), ())), preferred_element_type=jnp.float32
        )
        * scale
    )
    sketch = chip_first_sum(sketch_term, ("dp_0", "dp_1"), "dp_2").astype(jnp.float32)
    basis = cholesky_pass(sketch, inner_gram(sketch)).astype(jnp.bfloat16)
    reduced = jnp.dot(features, basis, preferred_element_type=jnp.float32).astype(jnp.bfloat16)
    shaped = jnp.dot(token_gram, reduced, preferred_element_type=jnp.float32).astype(jnp.bfloat16)
    core_term = (
        lax.dot_general(
            reduced, shaped, (((0,), (0,)), ((), ())), preferred_element_type=jnp.float32
        )
        * scale
    )
    core_matrix = ring_sum(butterfly_sum(core_term, DP, (1, 16)), "dp_1")
    shifted = core_matrix + jnp.eye(core_matrix.shape[0], dtype=jnp.float32)
    inverse = inverse_factor(shifted)
    factor = mm(inverse.T, mm(inverse, core_matrix))
    blocks = spread(momentum, "blk")
    columns = blocks.reshape(-1, blocks.shape[-1])
    coeffs = lax.dot_general(
        basis, columns, (((0,), (0,)), ((), ())), preferred_element_type=jnp.float32
    )
    scaled = jnp.dot(factor, coeffs, precision=lax.Precision.HIGHEST).astype(jnp.bfloat16)
    fresh = (
        columns.astype(jnp.float32) - jnp.dot(basis, scaled, preferred_element_type=jnp.float32)
    ).astype(jnp.bfloat16)
    return spread(fresh.reshape(blocks.shape), "blk")


def solution(mesh):
    torus = Mesh(mesh.devices.reshape(2, 8, 2, mesh.shape["blk"]), ("dp_0", "dp_1", "dp_2", "blk"))
    in_specs = (P("blk", DP, None), P("blk", DP, None), P("blk", None, None), P(None, "blk", DP))
    out_specs = P(None, "blk", DP)
    return jax.shard_map(
        shards, mesh=torus, in_specs=in_specs, out_specs=out_specs, check_vma=False
    )
```

```python
import functools
import jax
import jax.numpy as jnp
from jax import lax
from jax.sharding import Mesh
from jax.sharding import PartitionSpec as P
from jax.experimental import pallas as pl
from jax.experimental.pallas import tpu as pltpu

DP = ("dp_0", "dp_1", "dp_2")


def filled_up(lines, devices):
    spare = -len(lines) % devices
    return jnp.pad(lines, [(0, spare)] + [(0, 0)] * (lines.ndim - 1))


def copy_for_each(x, axis):
    devices = lax.axis_size(axis)
    return lax.all_to_all(jnp.broadcast_to(x[None], (devices, *x.shape)), axis, 0, 0, tiled=True)


def in_order(blocks, dim):
    blocks = jnp.moveaxis(blocks, 0, dim)
    lengths = blocks.shape
    return blocks.reshape(*lengths[:dim], lengths[dim] * lengths[dim + 1], *lengths[dim + 2 :])


def whole_of(x, axes, dim):
    far, near = axes
    first = copy_for_each(x, far)
    blocks = jnp.swapaxes(copy_for_each(first, near), 0, 1)
    return in_order(blocks.reshape(-1, *x.shape), dim)


def in_blocks(x, dim, devices):
    lengths = x.shape
    blocks = x.reshape(*lengths[:dim], devices, lengths[dim] // devices, *lengths[dim + 1 :])
    return jnp.moveaxis(blocks, dim, 0)


def sum_at_owner(x, axis, dim):
    blocks = in_blocks(x, dim, lax.axis_size(axis))
    arrived = lax.all_to_all(blocks, axis, split_axis=0, concat_axis=0, tiled=True)
    return arrived.sum(axis=0)


def sum_by_axis(x, axes, dim):
    far, near = axes
    blocks = in_blocks(x, dim, lax.axis_size(far))
    nearer = sum_at_owner(blocks, near, dim + 1).astype(jnp.bfloat16)
    arrived = lax.all_to_all(nearer, far, split_axis=0, concat_axis=0, tiled=True)
    return arrived.astype(jnp.float32).sum(axis=0)


def total_of(x, axes):
    lines = x.reshape(-1, x.shape[-1])
    padded = filled_up(lines, lax.axis_size(axes[0]) * lax.axis_size(axes[1]))
    whole = whole_of(sum_by_axis(padded, axes, 0).astype(jnp.bfloat16), axes, 0)
    return lax.slice_in_dim(whole, 0, len(lines)).reshape(x.shape)


def chip_first_sum(x, far, near):
    halves = x.reshape(lax.axis_size(near), -1, x.shape[-1])
    crossed = lax.all_to_all(halves.astype(jnp.bfloat16), near, split_axis=0, concat_axis=0, tiled=True)
    nearer = crossed.astype(jnp.float32).sum(axis=0)
    blocks = in_blocks(nearer, 0, lax.axis_size(far)).astype(jnp.bfloat16)
    arrived = lax.all_to_all(blocks, far, split_axis=0, concat_axis=0, tiled=True)
    own = arrived.astype(jnp.float32).sum(axis=0).astype(jnp.bfloat16)
    first = copy_for_each(own, far)
    return in_order(copy_for_each(first, near).reshape(-1, *own.shape), 0)


def collect(x, axis, dim):
    blocks = copy_for_each(x, axis)
    return in_order(blocks, dim)


def total_of_2(x, axes):
    lines = x.reshape(-1, x.shape[-1])
    own = sum_at_owner(filled_up(lines, lax.axis_size(axes)), axes, 0)
    whole = collect(own, axes, 0)
    return whole[: len(lines)].reshape(x.shape)


def butterfly_sum(x, axes, masks):
    size = 1
    for a in axes:
        size *= lax.axis_size(a)
    for m in masks:
        x = x + lax.ppermute(x, axes, [(i, i ^ m) for i in range(size)])
    return x


def shifted(x, axis, s):
    n = lax.axis_size(axis)
    return lax.ppermute(x, axis, [(j, (j + s) % n) for j in range(n)])


def spread(stack, axis):
    n = lax.axis_size(axis)
    me = lax.axis_index(axis)
    mine = jnp.roll(stack, -me, axis=0)
    pieces = [mine[0]] + [shifted(mine[s], axis, s) for s in range(1, n)]
    ordered = jnp.stack([pieces[(-i) % n] for i in range(n)])
    return jnp.roll(ordered, me, axis=0)


def gather_all(x, axis):
    n = lax.axis_size(axis)
    me = lax.axis_index(axis)
    pieces = [x] + [shifted(x, axis, s) for s in range(1, n)]
    ordered = jnp.stack([pieces[(-i) % n] for i in range(n)])
    return jnp.roll(ordered, me, axis=0)


def ring_sum(x, axis):
    n = lax.axis_size(axis)
    parts = x.reshape(n, x.shape[0] // n, *x.shape[1:])
    own = lax.all_to_all(parts, axis, 0, 0, tiled=True).sum(axis=0)
    return collect(own, axis, 0)


def inner_gram(columns):
    return lax.dot_general(
        columns, columns, (((0,), (0,)), ((), ())), precision=lax.Precision.HIGHEST
    )


def mm(a, b):
    return jnp.dot(a, b, precision=lax.Precision.HIGHEST)


def _factor_kernel(a_ref, w_ref, r_ref, panel_rows):
    n = a_ref.shape[0]
    rows_i = lax.broadcasted_iota(jnp.int32, (n, n), 0)
    cols_i = lax.broadcasted_iota(jnp.int32, (n, n), 1)
    r_ref[:, :n] = a_ref[...]
    r_ref[:, n:] = jnp.where(rows_i == cols_i, 1.0, 0.0).astype(jnp.float32)
    sub = lax.broadcasted_iota(jnp.int32, (panel_rows, 1), 0)
    lane_wide = lax.broadcasted_iota(jnp.int32, (1, 2 * n), 1)
    for p in range(n // panel_rows):
        r0 = panel_rows * p
        panel = r_ref[r0:r0 + panel_rows, :]
        for r in range(panel_rows):
            j = r0 + r
            part = panel[:, (j // 128) * 128:(j // 128 + 1) * 128]
            column = part[:, j % 128:j % 128 + 1]
            inv = lax.rsqrt(column[r:r + 1, :])
            row = jnp.where(lane_wide < j, 0.0, panel[r:r + 1, :] * inv)
            mult = jnp.where(sub > r, column * inv, 0.0)
            panel = jnp.where(sub == r, row, panel - mult * row)
        r_ref[r0:r0 + panel_rows, :] = panel
        low = r0 + panel_rows
        if low < n:
            outer = lax.dot_general(
                panel[:, :n], panel, (((0,), (0,)), ((), ())),
                precision=lax.Precision.HIGHEST, preferred_element_type=jnp.float32,
            )
            r_ref[low:, :] = r_ref[low:, :] - outer[low:, :]
    w_ref[...] = r_ref[:, n:]


def inverse_factor(matrix):
    n = matrix.shape[0]
    sym = (matrix + matrix.T) * 0.5
    return pl.pallas_call(
        functools.partial(_factor_kernel, panel_rows=64),
        out_shape=jax.ShapeDtypeStruct((n, n), jnp.float32),
        scratch_shapes=[pltpu.VMEM((n, 2 * n), jnp.float32)],
    )(sym)


def cholesky_pass(columns, gram_matrix):
    return mm(columns, inverse_factor(gram_matrix).T)


def shards(inputs, out_grads, test_matrix, momentum):
    features = inputs[0]
    errors = out_grads[0]
    probes = test_matrix[0]
    replicas = lax.axis_size(DP)
    scale = 1.0 / (features.shape[1] * features.shape[0] * replicas)
    projected = jnp.dot(features, probes, preferred_element_type=jnp.float32).astype(jnp.bfloat16)
    token_gram = lax.dot_general(
        errors, errors, (((1,), (1,)), ((), ())), preferred_element_type=jnp.float32
    ).astype(jnp.bfloat16)
    mixed_rows = jnp.dot(token_gram, projected, preferred_element_type=jnp.float32).astype(
        jnp.bfloat16
    )
    sketch_term = (
        lax.dot_general(
            features, mixed_rows, (((0,), (0,)), ((), ())), preferred_element_type=jnp.float32
        )
        * scale
    )
    sketch = chip_first_sum(sketch_term, ("dp_0", "dp_1"), "dp_2").astype(jnp.float32)
    basis = cholesky_pass(sketch, inner_gram(sketch)).astype(jnp.bfloat16)
    reduced = jnp.dot(features, basis, preferred_element_type=jnp.float32).astype(jnp.bfloat16)
    shaped = jnp.dot(token_gram, reduced, preferred_element_type=jnp.float32).astype(jnp.bfloat16)
    core_term = (
        lax.dot_general(
            reduced, shaped, (((0,), (0,)), ((), ())), preferred_element_type=jnp.float32
        )
        * scale
    )
    core_matrix = ring_sum(butterfly_sum(core_term, DP, (1, 16)), "dp_1")
    shifted = core_matrix + jnp.eye(core_matrix.shape[0], dtype=jnp.float32)
    inverse = inverse_factor(shifted)
    factor = mm(inverse.T, mm(inverse, core_matrix))
    blocks = spread(momentum, "blk")
    columns = blocks.reshape(-1, blocks.shape[-1])
    coeffs = lax.dot_general(
        basis, columns, (((0,), (0,)), ((), ())), preferred_element_type=jnp.float32
    )
    scaled = jnp.dot(factor, coeffs, precision=lax.Precision.HIGHEST).astype(jnp.bfloat16)
    fresh = (
        columns.astype(jnp.float32) - jnp.dot(basis, scaled, preferred_element_type=jnp.float32)
    ).astype(jnp.bfloat16)
    return spread(fresh.reshape(blocks.shape), "blk")


def solution(mesh):
    torus = Mesh(mesh.devices.reshape(2, 8, 2, mesh.shape["blk"]), ("dp_0", "dp_1", "dp_2", "blk"))
    in_specs = (P("blk", DP, None), P("blk", DP, None), P("blk", None, None), P(None, "blk", DP))
    out_specs = P(None, "blk", DP)
    return jax.shard_map(
        shards, mesh=torus, in_specs=in_specs, out_specs=out_specs, check_vma=False
    )
```

```python
import functools
import jax
import jax.numpy as jnp
from jax import lax
from jax.sharding import Mesh
from jax.sharding import PartitionSpec as P
from jax.experimental import pallas as pl
from jax.experimental.pallas import tpu as pltpu

DP = ("dp_0", "dp_1", "dp_2")


def filled_up(lines, devices):
    spare = -len(lines) % devices
    return jnp.pad(lines, [(0, spare)] + [(0, 0)] * (lines.ndim - 1))


def copy_for_each(x, axis):
    devices = lax.axis_size(axis)
    return lax.all_to_all(jnp.broadcast_to(x[None], (devices, *x.shape)), axis, 0, 0, tiled=True)


def in_order(blocks, dim):
    blocks = jnp.moveaxis(blocks, 0, dim)
    lengths = blocks.shape
    return blocks.reshape(*lengths[:dim], lengths[dim] * lengths[dim + 1], *lengths[dim + 2 :])


def whole_of(x, axes, dim):
    far, near = axes
    first = copy_for_each(x, far)
    blocks = jnp.swapaxes(copy_for_each(first, near), 0, 1)
    return in_order(blocks.reshape(-1, *x.shape), dim)


def in_blocks(x, dim, devices):
    lengths = x.shape
    blocks = x.reshape(*lengths[:dim], devices, lengths[dim] // devices, *lengths[dim + 1 :])
    return jnp.moveaxis(blocks, dim, 0)


def sum_at_owner(x, axis, dim):
    blocks = in_blocks(x, dim, lax.axis_size(axis))
    arrived = lax.all_to_all(blocks, axis, split_axis=0, concat_axis=0, tiled=True)
    return arrived.sum(axis=0)


def sum_by_axis(x, axes, dim):
    far, near = axes
    blocks = in_blocks(x, dim, lax.axis_size(far))
    nearer = sum_at_owner(blocks, near, dim + 1).astype(jnp.bfloat16)
    arrived = lax.all_to_all(nearer, far, split_axis=0, concat_axis=0, tiled=True)
    return arrived.astype(jnp.float32).sum(axis=0)


def total_of(x, axes):
    lines = x.reshape(-1, x.shape[-1])
    padded = filled_up(lines, lax.axis_size(axes[0]) * lax.axis_size(axes[1]))
    whole = whole_of(sum_by_axis(padded, axes, 0).astype(jnp.bfloat16), axes, 0)
    return lax.slice_in_dim(whole, 0, len(lines)).reshape(x.shape)


def chip_first_sum(x, far, near):
    halves = x.reshape(lax.axis_size(near), -1, x.shape[-1])
    crossed = lax.all_to_all(halves.astype(jnp.bfloat16), near, split_axis=0, concat_axis=0, tiled=True)
    nearer = crossed.astype(jnp.float32).sum(axis=0)
    blocks = in_blocks(nearer, 0, lax.axis_size(far)).astype(jnp.bfloat16)
    arrived = lax.all_to_all(blocks, far, split_axis=0, concat_axis=0, tiled=True)
    own = arrived.astype(jnp.float32).sum(axis=0).astype(jnp.bfloat16)
    first = copy_for_each(own, far)
    return in_order(copy_for_each(first, near).reshape(-1, *own.shape), 0)


def collect(x, axis, dim):
    blocks = copy_for_each(x, axis)
    return in_order(blocks, dim)


def total_of_2(x, axes):
    lines = x.reshape(-1, x.shape[-1])
    own = sum_at_owner(filled_up(lines, lax.axis_size(axes)), axes, 0)
    whole = collect(own, axes, 0)
    return whole[: len(lines)].reshape(x.shape)


def butterfly_sum(x, axes, masks):
    size = 1
    for a in axes:
        size *= lax.axis_size(a)
    for m in masks:
        sent = x.astype(jnp.bfloat16)
        x = sent.astype(jnp.float32) + lax.ppermute(sent, axes, [(i, i ^ m) for i in range(size)]).astype(jnp.float32)
    return x


def shifted(x, axis, s):
    n = lax.axis_size(axis)
    return lax.ppermute(x, axis, [(j, (j + s) % n) for j in range(n)])


def spread(stack, axis):
    n = lax.axis_size(axis)
    me = lax.axis_index(axis)
    mine = jnp.roll(stack, -me, axis=0)
    pieces = [mine[0]] + [shifted(mine[s], axis, s) for s in range(1, n)]
    ordered = jnp.stack([pieces[(-i) % n] for i in range(n)])
    return jnp.roll(ordered, me, axis=0)


def gather_all(x, axis):
    n = lax.axis_size(axis)
    me = lax.axis_index(axis)
    pieces = [x] + [shifted(x, axis, s) for s in range(1, n)]
    ordered = jnp.stack([pieces[(-i) % n] for i in range(n)])
    return jnp.roll(ordered, me, axis=0)


def ring_sum(x, axis):
    n = lax.axis_size(axis)
    parts = x.reshape(n, x.shape[0] // n, *x.shape[1:])
    own = lax.all_to_all(parts.astype(jnp.bfloat16), axis, 0, 0, tiled=True).astype(jnp.float32).sum(axis=0)
    return collect(own.astype(jnp.bfloat16), axis, 0).astype(jnp.float32)


def inner_gram(columns):
    return lax.dot_general(
        columns, columns, (((0,), (0,)), ((), ())), precision=lax.Precision.HIGHEST
    )


def mm(a, b):
    return jnp.dot(a, b, precision=lax.Precision.HIGHEST)


def _factor_kernel(a_ref, w_ref, r_ref, panel_rows):
    n = a_ref.shape[0]
    rows_i = lax.broadcasted_iota(jnp.int32, (n, n), 0)
    cols_i = lax.broadcasted_iota(jnp.int32, (n, n), 1)
    r_ref[:, :n] = a_ref[...]
    r_ref[:, n:] = jnp.where(rows_i == cols_i, 1.0, 0.0).astype(jnp.float32)
    sub = lax.broadcasted_iota(jnp.int32, (panel_rows, 1), 0)
    lane_wide = lax.broadcasted_iota(jnp.int32, (1, 2 * n), 1)
    for p in range(n // panel_rows):
        r0 = panel_rows * p
        panel = r_ref[r0:r0 + panel_rows, :]
        for r in range(panel_rows):
            j = r0 + r
            part = panel[:, (j // 128) * 128:(j // 128 + 1) * 128]
            column = part[:, j % 128:j % 128 + 1]
            inv = lax.rsqrt(column[r:r + 1, :])
            row = jnp.where(lane_wide < j, 0.0, panel[r:r + 1, :] * inv)
            mult = jnp.where(sub > r, column * inv, 0.0)
            panel = jnp.where(sub == r, row, panel - mult * row)
        r_ref[r0:r0 + panel_rows, :] = panel
        low = r0 + panel_rows
        if low < n:
            outer = lax.dot_general(
                panel[:, :n], panel, (((0,), (0,)), ((), ())),
                precision=lax.Precision.HIGHEST, preferred_element_type=jnp.float32,
            )
            r_ref[low:, :] = r_ref[low:, :] - outer[low:, :]
    w_ref[...] = r_ref[:, n:]


def inverse_factor(matrix):
    n = matrix.shape[0]
    sym = (matrix + matrix.T) * 0.5
    return pl.pallas_call(
        functools.partial(_factor_kernel, panel_rows=64),
        out_shape=jax.ShapeDtypeStruct((n, n), jnp.float32),
        scratch_shapes=[pltpu.VMEM((n, 2 * n), jnp.float32)],
    )(sym)


def cholesky_pass(columns, gram_matrix):
    return mm(columns, inverse_factor(gram_matrix).T)


def shards(inputs, out_grads, test_matrix, momentum):
    features = inputs[0]
    errors = out_grads[0]
    probes = test_matrix[0]
    replicas = lax.axis_size(DP)
    scale = 1.0 / (features.shape[1] * features.shape[0] * replicas)
    projected = jnp.dot(features, probes, preferred_element_type=jnp.float32).astype(jnp.bfloat16)
    token_gram = lax.dot_general(
        errors, errors, (((1,), (1,)), ((), ())), preferred_element_type=jnp.float32
    ).astype(jnp.bfloat16)
    mixed_rows = jnp.dot(token_gram, projected, preferred_element_type=jnp.float32).astype(
        jnp.bfloat16
    )
    sketch_term = (
        lax.dot_general(
            features, mixed_rows, (((0,), (0,)), ((), ())), preferred_element_type=jnp.float32
        )
        * scale
    )
    sketch = chip_first_sum(sketch_term, ("dp_0", "dp_1"), "dp_2").astype(jnp.float32)
    basis = cholesky_pass(sketch, inner_gram(sketch)).astype(jnp.bfloat16)
    reduced = jnp.dot(features, basis, preferred_element_type=jnp.float32).astype(jnp.bfloat16)
    shaped = jnp.dot(token_gram, reduced, preferred_element_type=jnp.float32).astype(jnp.bfloat16)
    core_term = (
        lax.dot_general(
            reduced, shaped, (((0,), (0,)), ((), ())), preferred_element_type=jnp.float32
        )
        * scale
    )
    core_matrix = ring_sum(butterfly_sum(core_term, DP, (1, 16)), "dp_1")
    shifted = core_matrix + jnp.eye(core_matrix.shape[0], dtype=jnp.float32)
    inverse = inverse_factor(shifted)
    factor = mm(inverse.T, mm(inverse, core_matrix))
    blocks = spread(momentum, "blk")
    columns = blocks.reshape(-1, blocks.shape[-1])
    coeffs = lax.dot_general(
        basis, columns, (((0,), (0,)), ((), ())), preferred_element_type=jnp.float32
    )
    scaled = jnp.dot(factor, coeffs, precision=lax.Precision.HIGHEST).astype(jnp.bfloat16)
    fresh = (
        columns.astype(jnp.float32) - jnp.dot(basis, scaled, preferred_element_type=jnp.float32)
    ).astype(jnp.bfloat16)
    return spread(fresh.reshape(blocks.shape), "blk")


def solution(mesh):
    torus = Mesh(mesh.devices.reshape(2, 8, 2, mesh.shape["blk"]), ("dp_0", "dp_1", "dp_2", "blk"))
    in_specs = (P("blk", DP, None), P("blk", DP, None), P("blk", None, None), P(None, "blk", DP))
    out_specs = P(None, "blk", DP)
    return jax.shard_map(
        shards, mesh=torus, in_specs=in_specs, out_specs=out_specs, check_vma=False
    )
```

```python
import functools
import jax
import jax.numpy as jnp
from jax import lax
from jax.sharding import Mesh
from jax.sharding import PartitionSpec as P
from jax.experimental import pallas as pl
from jax.experimental.pallas import tpu as pltpu

DP = ("dp_0", "dp_1", "dp_2")


def filled_up(lines, devices):
    spare = -len(lines) % devices
    return jnp.pad(lines, [(0, spare)] + [(0, 0)] * (lines.ndim - 1))


def copy_for_each(x, axis):
    devices = lax.axis_size(axis)
    return lax.all_to_all(jnp.broadcast_to(x[None], (devices, *x.shape)), axis, 0, 0, tiled=True)


def in_order(blocks, dim):
    blocks = jnp.moveaxis(blocks, 0, dim)
    lengths = blocks.shape
    return blocks.reshape(*lengths[:dim], lengths[dim] * lengths[dim + 1], *lengths[dim + 2 :])


def whole_of(x, axes, dim):
    far, near = axes
    first = copy_for_each(x, far)
    blocks = jnp.swapaxes(copy_for_each(first, near), 0, 1)
    return in_order(blocks.reshape(-1, *x.shape), dim)


def in_blocks(x, dim, devices):
    lengths = x.shape
    blocks = x.reshape(*lengths[:dim], devices, lengths[dim] // devices, *lengths[dim + 1 :])
    return jnp.moveaxis(blocks, dim, 0)


def sum_at_owner(x, axis, dim):
    blocks = in_blocks(x, dim, lax.axis_size(axis))
    arrived = lax.all_to_all(blocks, axis, split_axis=0, concat_axis=0, tiled=True)
    return arrived.sum(axis=0)


def sum_by_axis(x, axes, dim):
    far, near = axes
    blocks = in_blocks(x, dim, lax.axis_size(far))
    nearer = sum_at_owner(blocks, near, dim + 1).astype(jnp.bfloat16)
    arrived = lax.all_to_all(nearer, far, split_axis=0, concat_axis=0, tiled=True)
    return arrived.astype(jnp.float32).sum(axis=0)


def total_of(x, axes):
    lines = x.reshape(-1, x.shape[-1])
    padded = filled_up(lines, lax.axis_size(axes[0]) * lax.axis_size(axes[1]))
    whole = whole_of(sum_by_axis(padded, axes, 0).astype(jnp.bfloat16), axes, 0)
    return lax.slice_in_dim(whole, 0, len(lines)).reshape(x.shape)


def chip_first_sum(x, far, near):
    halves = x.reshape(lax.axis_size(near), -1, x.shape[-1])
    crossed = lax.all_to_all(halves.astype(jnp.bfloat16), near, split_axis=0, concat_axis=0, tiled=True)
    nearer = crossed.astype(jnp.float32).sum(axis=0)
    blocks = in_blocks(nearer, 0, lax.axis_size(far)).astype(jnp.bfloat16)
    arrived = lax.all_to_all(blocks, far, split_axis=0, concat_axis=0, tiled=True)
    own = arrived.astype(jnp.float32).sum(axis=0).astype(jnp.bfloat16)
    first = copy_for_each(own, far)
    return in_order(copy_for_each(first, near).reshape(-1, *own.shape), 0)


def collect(x, axis, dim):
    blocks = copy_for_each(x, axis)
    return in_order(blocks, dim)


def total_of_2(x, axes):
    lines = x.reshape(-1, x.shape[-1])
    own = sum_at_owner(filled_up(lines, lax.axis_size(axes)), axes, 0)
    whole = collect(own, axes, 0)
    return whole[: len(lines)].reshape(x.shape)


def butterfly_sum(x, axes, masks):
    size = 1
    for a in axes:
        size *= lax.axis_size(a)
    for m in masks:
        sent = x.astype(jnp.bfloat16)
        x = sent.astype(jnp.float32) + lax.ppermute(sent, axes, [(i, i ^ m) for i in range(size)]).astype(jnp.float32)
    return x


def shifted(x, axis, s):
    n = lax.axis_size(axis)
    return lax.ppermute(x, axis, [(j, (j + s) % n) for j in range(n)])


def spread(stack, axis):
    n = lax.axis_size(axis)
    me = lax.axis_index(axis)
    mine = jnp.roll(stack, -me, axis=0)
    pieces = [mine[0]] + [shifted(mine[s], axis, s) for s in range(1, n)]
    ordered = jnp.stack([pieces[(-i) % n] for i in range(n)])
    return jnp.roll(ordered, me, axis=0)


def gather_all(x, axis):
    n = lax.axis_size(axis)
    me = lax.axis_index(axis)
    pieces = [x] + [shifted(x, axis, s) for s in range(1, n)]
    ordered = jnp.stack([pieces[(-i) % n] for i in range(n)])
    return jnp.roll(ordered, me, axis=0)


def ring_sum(x, axis):
    n = lax.axis_size(axis)
    parts = x.reshape(n, x.shape[0] // n, *x.shape[1:])
    own = lax.all_to_all(parts.astype(jnp.bfloat16), axis, 0, 0, tiled=True).astype(jnp.float32).sum(axis=0)
    return collect(own.astype(jnp.bfloat16), axis, 0).astype(jnp.float32)


def inner_gram(columns):
    return lax.dot_general(
        columns, columns, (((0,), (0,)), ((), ())), precision=lax.Precision.HIGHEST
    )


def mm(a, b):
    return jnp.dot(a, b, precision=lax.Precision.HIGHEST)


def _factor_kernel(a_ref, w_ref, r_ref, panel_rows):
    n = a_ref.shape[0]
    rows_i = lax.broadcasted_iota(jnp.int32, (n, n), 0)
    cols_i = lax.broadcasted_iota(jnp.int32, (n, n), 1)
    r_ref[:, :n] = a_ref[...]
    r_ref[:, n:] = jnp.where(rows_i == cols_i, 1.0, 0.0).astype(jnp.float32)
    sub = lax.broadcasted_iota(jnp.int32, (panel_rows, 1), 0)
    lane_wide = lax.broadcasted_iota(jnp.int32, (1, 2 * n), 1)
    for p in range(n // panel_rows):
        r0 = panel_rows * p
        panel = r_ref[r0:r0 + panel_rows, :]
        for r in range(panel_rows):
            j = r0 + r
            part = panel[:, (j // 128) * 128:(j // 128 + 1) * 128]
            column = part[:, j % 128:j % 128 + 1]
            inv = lax.rsqrt(column[r:r + 1, :])
            row = jnp.where(lane_wide < j, 0.0, panel[r:r + 1, :] * inv)
            mult = jnp.where(sub > r, column * inv, 0.0)
            panel = jnp.where(sub == r, row, panel - mult * row)
        r_ref[r0:r0 + panel_rows, :] = panel
        low = r0 + panel_rows
        if low < n:
            outer = lax.dot_general(
                panel[:, :n], panel, (((0,), (0,)), ((), ())),
                precision=lax.Precision.HIGHEST, preferred_element_type=jnp.float32,
            )
            r_ref[low:, :] = r_ref[low:, :] - outer[low:, :]
    w_ref[...] = r_ref[:, n:]


def inverse_factor(matrix):
    n = matrix.shape[0]
    sym = (matrix + matrix.T) * 0.5
    return pl.pallas_call(
        functools.partial(_factor_kernel, panel_rows=64),
        out_shape=jax.ShapeDtypeStruct((n, n), jnp.float32),
        scratch_shapes=[pltpu.VMEM((n, 2 * n), jnp.float32)],
    )(sym)


def cholesky_pass(columns, gram_matrix):
    return mm(columns, inverse_factor(gram_matrix).T)


def shards(inputs, out_grads, test_matrix, momentum):
    features = inputs[0]
    errors = out_grads[0]
    probes = test_matrix[0]
    replicas = lax.axis_size(DP)
    scale = 1.0 / (features.shape[1] * features.shape[0] * replicas)
    projected = jnp.dot(features, probes, preferred_element_type=jnp.float32).astype(jnp.bfloat16)
    token_gram = lax.dot_general(
        errors, errors, (((1,), (1,)), ((), ())), preferred_element_type=jnp.float32
    ).astype(jnp.bfloat16)
    mixed_rows = jnp.dot(token_gram, projected, preferred_element_type=jnp.float32).astype(
        jnp.bfloat16
    )
    sketch_term = (
        lax.dot_general(
            features, mixed_rows, (((0,), (0,)), ((), ())), preferred_element_type=jnp.float32
        )
        * scale
    )
    arrived = chip_first_sum(sketch_term, ("dp_0", "dp_1"), "dp_2")
    gram = lax.dot_general(
        arrived, arrived, (((0,), (0,)), ((), ())), preferred_element_type=jnp.float32
    )
    basis = cholesky_pass(arrived.astype(jnp.float32), gram).astype(jnp.bfloat16)
    reduced = jnp.dot(features, basis, preferred_element_type=jnp.float32).astype(jnp.bfloat16)
    shaped = jnp.dot(token_gram, reduced, preferred_element_type=jnp.float32).astype(jnp.bfloat16)
    core_term = (
        lax.dot_general(
            reduced, shaped, (((0,), (0,)), ((), ())), preferred_element_type=jnp.float32
        )
        * scale
    )
    core_matrix = ring_sum(butterfly_sum(core_term, DP, (1, 16)), "dp_1")
    shifted = core_matrix + jnp.eye(core_matrix.shape[0], dtype=jnp.float32)
    inverse = inverse_factor(shifted)
    factor = mm(inverse.T, mm(inverse, core_matrix))
    blocks = spread(momentum, "blk")
    columns = blocks.reshape(-1, blocks.shape[-1])
    coeffs = lax.dot_general(
        basis, columns, (((0,), (0,)), ((), ())), preferred_element_type=jnp.float32
    )
    scaled = jnp.dot(factor, coeffs, precision=lax.Precision.HIGHEST).astype(jnp.bfloat16)
    fresh = (
        columns.astype(jnp.float32) - jnp.dot(basis, scaled, preferred_element_type=jnp.float32)
    ).astype(jnp.bfloat16)
    return spread(fresh.reshape(blocks.shape), "blk")


def solution(mesh):
    torus = Mesh(mesh.devices.reshape(2, 8, 2, mesh.shape["blk"]), ("dp_0", "dp_1", "dp_2", "blk"))
    in_specs = (P("blk", DP, None), P("blk", DP, None), P("blk", None, None), P(None, "blk", DP))
    out_specs = P(None, "blk", DP)
    return jax.shard_map(
        shards, mesh=torus, in_specs=in_specs, out_specs=out_specs, check_vma=False
    )
```

```python
import functools
import jax
import jax.numpy as jnp
from jax import lax
from jax.sharding import Mesh
from jax.sharding import PartitionSpec as P
from jax.experimental import pallas as pl
from jax.experimental.pallas import tpu as pltpu

DP = ("dp_0", "dp_1", "dp_2")


def filled_up(lines, devices):
    spare = -len(lines) % devices
    return jnp.pad(lines, [(0, spare)] + [(0, 0)] * (lines.ndim - 1))


def copy_for_each(x, axis):
    devices = lax.axis_size(axis)
    return lax.all_to_all(jnp.broadcast_to(x[None], (devices, *x.shape)), axis, 0, 0, tiled=True)


def in_order(blocks, dim):
    blocks = jnp.moveaxis(blocks, 0, dim)
    lengths = blocks.shape
    return blocks.reshape(*lengths[:dim], lengths[dim] * lengths[dim + 1], *lengths[dim + 2 :])


def whole_of(x, axes, dim):
    far, near = axes
    first = copy_for_each(x, far)
    blocks = jnp.swapaxes(copy_for_each(first, near), 0, 1)
    return in_order(blocks.reshape(-1, *x.shape), dim)


def in_blocks(x, dim, devices):
    lengths = x.shape
    blocks = x.reshape(*lengths[:dim], devices, lengths[dim] // devices, *lengths[dim + 1 :])
    return jnp.moveaxis(blocks, dim, 0)


def sum_at_owner(x, axis, dim):
    blocks = in_blocks(x, dim, lax.axis_size(axis))
    arrived = lax.all_to_all(blocks, axis, split_axis=0, concat_axis=0, tiled=True)
    return arrived.sum(axis=0)


def sum_by_axis(x, axes, dim):
    far, near = axes
    blocks = in_blocks(x, dim, lax.axis_size(far))
    nearer = sum_at_owner(blocks, near, dim + 1).astype(jnp.bfloat16)
    arrived = lax.all_to_all(nearer, far, split_axis=0, concat_axis=0, tiled=True)
    return arrived.astype(jnp.float32).sum(axis=0)


def total_of(x, axes):
    lines = x.reshape(-1, x.shape[-1])
    padded = filled_up(lines, lax.axis_size(axes[0]) * lax.axis_size(axes[1]))
    whole = whole_of(sum_by_axis(padded, axes, 0).astype(jnp.bfloat16), axes, 0)
    return lax.slice_in_dim(whole, 0, len(lines)).reshape(x.shape)


def chip_first_sum(x, far, near):
    halves = x.reshape(lax.axis_size(near), -1, x.shape[-1])
    crossed = lax.all_to_all(halves.astype(jnp.bfloat16), near, split_axis=0, concat_axis=0, tiled=True)
    nearer = crossed.astype(jnp.float32).sum(axis=0)
    blocks = in_blocks(nearer, 0, lax.axis_size(far)).astype(jnp.bfloat16)
    arrived = lax.all_to_all(blocks, far, split_axis=0, concat_axis=0, tiled=True)
    own = arrived.astype(jnp.float32).sum(axis=0).astype(jnp.bfloat16)
    first = copy_for_each(own, far)
    return in_order(copy_for_each(first, near).reshape(-1, *own.shape), 0)


def collect(x, axis, dim):
    blocks = copy_for_each(x, axis)
    return in_order(blocks, dim)


def total_of_2(x, axes):
    lines = x.reshape(-1, x.shape[-1])
    own = sum_at_owner(filled_up(lines, lax.axis_size(axes)), axes, 0)
    whole = collect(own, axes, 0)
    return whole[: len(lines)].reshape(x.shape)


def butterfly_sum(x, axes, masks):
    size = 1
    for a in axes:
        size *= lax.axis_size(a)
    for m in masks:
        sent = x.astype(jnp.bfloat16)
        x = sent.astype(jnp.float32) + lax.ppermute(sent, axes, [(i, i ^ m) for i in range(size)]).astype(jnp.float32)
    return x


def shifted(x, axis, s):
    n = lax.axis_size(axis)
    return lax.ppermute(x, axis, [(j, (j + s) % n) for j in range(n)])


def spread(stack, axis):
    n = lax.axis_size(axis)
    me = lax.axis_index(axis)
    mine = jnp.roll(stack, -me, axis=0)
    pieces = [mine[0]] + [shifted(mine[s], axis, s) for s in range(1, n)]
    ordered = jnp.stack([pieces[(-i) % n] for i in range(n)])
    return jnp.roll(ordered, me, axis=0)


def gather_all(x, axis):
    n = lax.axis_size(axis)
    me = lax.axis_index(axis)
    pieces = [x] + [shifted(x, axis, s) for s in range(1, n)]
    ordered = jnp.stack([pieces[(-i) % n] for i in range(n)])
    return jnp.roll(ordered, me, axis=0)


def ring_sum(x, axis):
    n = lax.axis_size(axis)
    parts = x.reshape(n, x.shape[0] // n, *x.shape[1:])
    own = lax.all_to_all(parts.astype(jnp.bfloat16), axis, 0, 0, tiled=True).astype(jnp.float32).sum(axis=0)
    return collect(own.astype(jnp.bfloat16), axis, 0).astype(jnp.float32)


def inner_gram(columns):
    return lax.dot_general(
        columns, columns, (((0,), (0,)), ((), ())), precision=lax.Precision.HIGHEST
    )


def mm(a, b):
    return jnp.dot(a, b, precision=lax.Precision.HIGHEST)


def _factor_kernel(a_ref, w_ref, r_ref, panel_rows):
    n = a_ref.shape[0]
    rows_i = lax.broadcasted_iota(jnp.int32, (n, n), 0)
    cols_i = lax.broadcasted_iota(jnp.int32, (n, n), 1)
    r_ref[:, :n] = a_ref[...]
    r_ref[:, n:] = jnp.where(rows_i == cols_i, 1.0, 0.0).astype(jnp.float32)
    sub = lax.broadcasted_iota(jnp.int32, (panel_rows, 1), 0)
    for p in range(n // panel_rows):
        r0 = panel_rows * p
        lo = (r0 // 128) * 128
        hi = n + ((r0 + panel_rows - 1) // 128 + 1) * 128
        lane_wide = lax.broadcasted_iota(jnp.int32, (1, hi - lo), 1) + lo
        panel = r_ref[r0:r0 + panel_rows, lo:hi]
        for r in range(panel_rows):
            j = r0 + r
            part = panel[:, (j // 128) * 128 - lo:(j // 128 + 1) * 128 - lo]
            column = part[:, j % 128:j % 128 + 1]
            inv = lax.rsqrt(column[r:r + 1, :])
            row = jnp.where(lane_wide < j, 0.0, panel[r:r + 1, :] * inv)
            mult = jnp.where(sub > r, column * inv, 0.0)
            panel = jnp.where(sub == r, row, panel - mult * row)
        r_ref[r0:r0 + panel_rows, lo:hi] = panel
        low = r0 + panel_rows
        if low < n:
            outer = lax.dot_general(
                r_ref[r0:r0 + panel_rows, :n], panel, (((0,), (0,)), ((), ())),
                precision=lax.Precision.HIGHEST, preferred_element_type=jnp.float32,
            )
            r_ref[low:, lo:hi] = r_ref[low:, lo:hi] - outer[low:, :]
    w_ref[...] = r_ref[:, n:]


def inverse_factor(matrix):
    n = matrix.shape[0]
    sym = (matrix + matrix.T) * 0.5
    return pl.pallas_call(
        functools.partial(_factor_kernel, panel_rows=128),
        out_shape=jax.ShapeDtypeStruct((n, n), jnp.float32),
        scratch_shapes=[pltpu.VMEM((n, 2 * n), jnp.float32)],
    )(sym)


def cholesky_pass(columns, gram_matrix):
    return mm(columns, inverse_factor(gram_matrix).T)


def shards(inputs, out_grads, test_matrix, momentum):
    features = inputs[0]
    errors = out_grads[0]
    probes = test_matrix[0]
    replicas = lax.axis_size(DP)
    scale = 1.0 / (features.shape[1] * features.shape[0] * replicas)
    projected = jnp.dot(features, probes, preferred_element_type=jnp.float32).astype(jnp.bfloat16)
    token_gram = lax.dot_general(
        errors, errors, (((1,), (1,)), ((), ())), preferred_element_type=jnp.float32
    ).astype(jnp.bfloat16)
    mixed_rows = jnp.dot(token_gram, projected, preferred_element_type=jnp.float32).astype(
        jnp.bfloat16
    )
    sketch_term = (
        lax.dot_general(
            features, mixed_rows, (((0,), (0,)), ((), ())), preferred_element_type=jnp.float32
        )
        * scale
    )
    sketch = chip_first_sum(sketch_term, ("dp_0", "dp_1"), "dp_2").astype(jnp.float32)
    basis = cholesky_pass(sketch, inner_gram(sketch)).astype(jnp.bfloat16)
    reduced = jnp.dot(features, basis, preferred_element_type=jnp.float32).astype(jnp.bfloat16)
    shaped = jnp.dot(token_gram, reduced, preferred_element_type=jnp.float32).astype(jnp.bfloat16)
    core_term = (
        lax.dot_general(
            reduced, shaped, (((0,), (0,)), ((), ())), preferred_element_type=jnp.float32
        )
        * scale
    )
    core_matrix = ring_sum(butterfly_sum(core_term, DP, (1, 16)), "dp_1")
    shifted = core_matrix + jnp.eye(core_matrix.shape[0], dtype=jnp.float32)
    inverse = inverse_factor(shifted)
    factor = mm(inverse.T, mm(inverse, core_matrix))
    blocks = spread(momentum, "blk")
    columns = blocks.reshape(-1, blocks.shape[-1])
    coeffs = lax.dot_general(
        basis, columns, (((0,), (0,)), ((), ())), preferred_element_type=jnp.float32
    )
    scaled = jnp.dot(factor, coeffs, precision=lax.Precision.HIGHEST).astype(jnp.bfloat16)
    fresh = (
        columns.astype(jnp.float32) - jnp.dot(basis, scaled, preferred_element_type=jnp.float32)
    ).astype(jnp.bfloat16)
    return spread(fresh.reshape(blocks.shape), "blk")


def solution(mesh):
    torus = Mesh(mesh.devices.reshape(2, 8, 2, mesh.shape["blk"]), ("dp_0", "dp_1", "dp_2", "blk"))
    in_specs = (P("blk", DP, None), P("blk", DP, None), P("blk", None, None), P(None, "blk", DP))
    out_specs = P(None, "blk", DP)
    return jax.shard_map(
        shards, mesh=torus, in_specs=in_specs, out_specs=out_specs, check_vma=False
    )
```
